512 devices in a mesh: req: 128 (over x, z, core), tp: 4 (over y).
Axes of the slice: x: 4, y: 4, z: 16, core: 2. Of those that a mesh axis runs over, the one named last changes fastest.
Arguments:
- queries: bfloat16 [1024, 4096], P('req', 'tp'), may hold values from -320 to 320, as said below
- new_kv: bfloat16 [1024, 2, 512], P('req', None, 'tp'), may hold values from -6 to 6
- own_kv: bfloat16 [1024, 128, 2, 512], P('req', None, None, 'tp'), may hold values from -6 to 6
- prompt_kv: bfloat16 [128, 512, 2, 512], P('req', None, None, 'tp'), may hold values from -6 to 6
- out_weight: bfloat16 [4096, 2048], P('tp'), may hold values from -0.09375 to 0.09375
- parents: int32 [1024], replicated, may hold values from 0 to 1023, as said below
- own_len: int32 [1024], replicated, may hold values from 1 to 128, as said below
- first_beam: int32 [1024], replicated, may hold values from 0 to 1023, as said below
Outputs:
- mixed_out: bfloat16 [1024, 2048], P('req', 'tp')
The draws below stay inside these ranges and needn't reach their ends.
Inputs may be any that keep to these rules, and one draw needn't show every extreme that they name: Beams of one request are consecutive; first_beam[b] is the first of them; every request but the last holds 8 to 16 beams, and one holds exactly 16. parents[b] is a beam of the same request as b. `own_len`: some beam has exactly 128 valid positions. queries are real-valued, with row scales that may differ widely.
All inputs are finite; a program needn't handle non-finite values.
Results may differ from the reference program's by a relative error of at most 0.015.
Values may be sent and summed in bfloat16 or wider, within the bound.
No kernel may reach another device: no remote copies, remote signals or barrier semaphores. Data moves between devices by JAX's collectives and lax.ppermute only.
A program may use at most 64 MiB of HBM per device.

```python
import jax
import jax.numpy as jnp
from jax import lax

H = 32
KVH = 4
HD = 128
W = 2048
BEAM_DEV = 8
MOST_BEAMS = 16
OWN_LEN = 128
PROMPT = 512
BEAMS = 1024
HOMES = 128


def request_layout(key):
    request_count = BEAMS // BEAM_DEV + 1
    request_sizes = jax.random.randint(jax.random.fold_in(key, 11), (request_count,), BEAM_DEV, MOST_BEAMS + 1).astype(jnp.int32)
    request_sizes = request_sizes.at[0].set(MOST_BEAMS)
    request_ends = jnp.cumsum(request_sizes).astype(jnp.int32)
    request_starts = request_ends - request_sizes
    position = jnp.arange(BEAMS, dtype=jnp.int32)
    request_idx = jnp.sum((request_ends[None, :] <= position[:, None]).astype(jnp.int32), axis=1)
    first_slot = request_starts[request_idx]
    span_size = jnp.minimum(request_sizes[request_idx], BEAMS - first_slot)
    return (first_slot, span_size)


def draw_first_beam(key, part):
    return request_layout(key)[0]


def draw_parents(key, part):
    first_slot, span_size = request_layout(key)
    steps_drawn = jax.random.randint(jax.random.fold_in(key, 23), (BEAMS,), 0, span_size)
    chosen = (first_slot + steps_drawn).astype(jnp.int32)
    chosen = chosen.at[0].set(0)
    chosen = chosen.at[BEAMS - 1].set(BEAMS - 1)
    return chosen.astype(jnp.int32)


def draw_own_len(key, part):
    device_caps = jax.random.randint(jax.random.fold_in(key, 31), (BEAMS // BEAM_DEV,), max(OWN_LEN // 4, 1), OWN_LEN + 1)
    caps_beam = jnp.repeat(device_caps, BEAM_DEV)
    lengths = jax.random.randint(jax.random.fold_in(key, 37), (BEAMS,), 1, caps_beam + 1)
    return lengths.at[0].set(OWN_LEN).astype(jnp.int32)


def draw_queries(key, part):
    values_drawn = jax.random.truncated_normal(key, -4.0, 4.0, (BEAMS, H * HD), jnp.float32)
    return values_drawn.astype(jnp.bfloat16)


def shard_levels(own_key, extent, shards, smallest, high):
    factor_of = 1.0
    for axis_at, shards_of in shards:
        draws = jax.random.uniform(jax.random.fold_in(jax.random.fold_in(own_key, 6), axis_at), (shards_of,), jnp.float32, smallest / len(shards), high / len(shards))
        factor_of = factor_of * jnp.repeat(jnp.exp(draws), extent[axis_at] // shards_of).reshape((-1,) + (1,) * (len(extent) - 1 - axis_at))
    return factor_of


def scatter_about(own_key, shape, width, bound, pieces=(), kind=jnp.bfloat16):
    values = width * jax.random.normal(own_key, shape, jnp.float32)
    if pieces:
        values = values * shard_levels(own_key, shape, pieces, -0.22, 0.18)
    return jnp.clip(values, -bound, bound).astype(kind)


def setup_inputs(seed: int = 0) -> dict:
    seeds = jax.random.split(jax.random.key(seed), 9)
    return {
        "queries": draw_queries(jax.random.fold_in(seeds[8], 71), 0),
        "new_kv": scatter_about(seeds[1], (BEAMS, 2, KVH * HD), 1.0, 6.0, ((0, 128), (2, 4))),
        "own_kv": scatter_about(seeds[2], (BEAMS, OWN_LEN, 2, KVH * HD), 1.0, 6.0, ((0, 128), (3, 4))),
        "prompt_kv": scatter_about(seeds[3], (HOMES, PROMPT, 2, KVH * HD), 1.0, 6.0, ((0, 128), (3, 4))),
        "out_weight": scatter_about(seeds[4], (H * HD, W), (H * HD) ** -0.5, 0.09375, ((0, 4),)),
        "parents": draw_parents(jax.random.fold_in(seeds[8], 71), 0),
        "own_len": draw_own_len(jax.random.fold_in(seeds[8], 71), 0),
        "first_beam": draw_first_beam(jax.random.fold_in(seeds[8], 71), 0),
    }


def reference(queries, new_kv, own_kv, prompt_kv, out_weight, parents, own_len, first_beam):
    score_scale = HD ** -0.5
    home_slots = (first_beam // BEAM_DEV).astype(jnp.int32)
    own_positions = jnp.arange(OWN_LEN, dtype=jnp.int32)

    def attend_beam(entries):
        query_row, parent, home_slot, fresh_row = entries
        key_rows = jnp.concatenate([prompt_kv[home_slot], own_kv[parent], fresh_row[None]], axis=0)
        allowed = jnp.concatenate([jnp.ones((PROMPT,), bool), own_positions < own_len[parent], jnp.ones((1,), bool)])
        keys_f = key_rows[:, 0].astype(jnp.float32).reshape(-1, KVH, HD)
        values_f = key_rows[:, 1].astype(jnp.float32).reshape(-1, KVH, HD)
        query_heads = query_row.astype(jnp.float32).reshape(KVH, H // KVH, HD)
        scores = jnp.einsum("kgd,skd->kgs", query_heads, keys_f, precision=lax.Precision.HIGHEST) * score_scale
        scores = jnp.where(allowed, scores, -1.0e30)
        weights = jax.nn.softmax(scores, axis=-1)
        attended = jnp.einsum("kgs,skd->kgd", weights, values_f, precision=lax.Precision.HIGHEST)
        return attended.reshape(H * HD).astype(jnp.bfloat16)

    attended_all = lax.map(attend_beam, (queries, parents, home_slots, new_kv))
    return jnp.dot(attended_all, out_weight, preferred_element_type=jnp.float32).astype(jnp.bfloat16)
```

```python
import jax
import jax.numpy as jnp
from jax import lax
from jax.sharding import PartitionSpec as P

HD = 128
MOST_BEAMS = 16


MASKED_SCORE = -1e30


def shifted(block, axis, distance):
    devices = range(lax.axis_size(axis))
    route = [(i + distance, i) for i in devices if i + distance in devices]
    return lax.ppermute(block, axis, route)


def split_weights(weights):
    high = weights.astype(jnp.bfloat16)
    low = (weights - high.astype(jnp.float32)).astype(jnp.bfloat16)
    return high, low


def partial_block(query_block, key_block, value_block, allowed):
    score_scale = query_block.shape[-1] ** (-0.5)
    scores = jnp.einsum(
        "nkgd,skd->nkgs", query_block, key_block, preferred_element_type=jnp.float32
    )
    scores = scores * score_scale
    masked = allowed[:, None, None, :]
    scores = jnp.where(masked, scores, MASKED_SCORE)
    peaks = jnp.max(scores, axis=-1)
    weights = jnp.where(masked, jnp.exp(scores - peaks[..., None]), 0.0)
    totals = jnp.sum(weights, axis=-1)
    high, low = split_weights(weights)
    formula = "nkgs,skd->nkgd"
    weighted = jnp.einsum(
        formula, high, value_block, preferred_element_type=jnp.float32
    ) + jnp.einsum(formula, low, value_block, preferred_element_type=jnp.float32)
    return (weighted, peaks, totals)


def merge_all(parts):
    peaks = [jnp.where(p[2] > 0, p[1], MASKED_SCORE) for p in parts]
    top = peaks[0]
    for pk in peaks[1:]:
        top = jnp.maximum(top, pk)
    weighted = 0.0
    totals = 0.0
    for part, pk in zip(parts, peaks):
        scale = jnp.where(part[2] > 0, jnp.exp(pk - top), 0.0)
        weighted = weighted + part[0] * scale[..., None]
        totals = totals + part[2] * scale
    return (weighted, top, totals)


def pack(part):
    weighted, peaks, totals = part
    n = weighted.shape[0]
    return jnp.concatenate(
        [weighted.reshape(n, -1), peaks.reshape(n, -1), totals.reshape(n, -1)], axis=1
    )


def unpack(packed, shape):
    n, k, g, d = shape
    width = k * g * d
    weighted = packed[:, :width].reshape(n, k, g, d)
    peaks = packed[:, width : width + k * g].reshape(n, k, g)
    totals = packed[:, width + k * g :].reshape(n, k, g)
    return (weighted, peaks, totals)


def local(queries, new_kv, own_kv, prompt_kv, out_weight, parents, own_len, first_beam):
    per_dev = queries.shape[0]
    head_dim = HD
    kv_heads_local = new_kv.shape[2] // head_dim
    q_heads_local = queries.shape[1] // head_dim
    group_size = q_heads_local // kv_heads_local
    own_size = own_kv.shape[1]
    prompt_size = prompt_kv.shape[1]
    req_count = lax.axis_size("req")
    beam_count = per_dev * req_count
    dev_index = lax.axis_index("req")
    reach_dev = (MOST_BEAMS - 2) // per_dev + 1
    offsets = list(range(-reach_dev, reach_dev + 1))
    shape4 = (per_dev, kv_heads_local, group_size, head_dim)

    query_block = queries.reshape(shape4)
    hood = [query_block if k == 0 else shifted(query_block, "req", k) for k in offsets]
    hood_queries = jnp.concatenate(hood, axis=0)
    hood_count = hood_queries.shape[0]
    hood_beams = (dev_index - reach_dev) * per_dev + jnp.arange(hood_count, dtype=jnp.int32)
    in_range = (hood_beams >= 0) & (hood_beams < beam_count)
    clipped = jnp.clip(hood_beams, 0, beam_count - 1)

    parent = parents[clipped]
    lengths = own_len[parent]
    parent_here = in_range & (parent // per_dev == dev_index)
    columns = jnp.arange(per_dev * own_size, dtype=jnp.int32)
    own_allowed = (
        parent_here[:, None]
        & (columns[None, :] // own_size == (parent % per_dev)[:, None])
        & (columns[None, :] % own_size < lengths[:, None])
    )
    own_keys = own_kv[:, :, 0].reshape(per_dev * own_size, kv_heads_local, head_dim)
    own_values = own_kv[:, :, 1].reshape(per_dev * own_size, kv_heads_local, head_dim)
    own_part = partial_block(hood_queries, own_keys, own_values, own_allowed)

    start = reach_dev * per_dev
    home_here = in_range[start:] & (first_beam[clipped[start:]] // per_dev == dev_index)
    prompt_allowed = jnp.broadcast_to(home_here[:, None], (hood_count - start, prompt_size))
    prompt_keys = prompt_kv[0, :, 0].reshape(prompt_size, kv_heads_local, head_dim)
    prompt_values = prompt_kv[0, :, 1].reshape(prompt_size, kv_heads_local, head_dim)
    prompt_part = partial_block(hood_queries[start:], prompt_keys, prompt_values, prompt_allowed)

    fresh_keys = new_kv[:, 0].reshape(per_dev, 1, kv_heads_local, head_dim)
    fresh_values = new_kv[:, 1].reshape(per_dev, 1, kv_heads_local, head_dim)
    fresh_scores = jnp.einsum(
        "nkgd,nskd->nkgs", query_block, fresh_keys, preferred_element_type=jnp.float32
    ) * (head_dim ** (-0.5))
    fresh_part = (
        fresh_values[:, 0, :, None, :].astype(jnp.float32) * jnp.ones_like(fresh_scores),
        fresh_scores[..., 0],
        jnp.ones_like(fresh_scores[..., 0]),
    )

    def block_of(part, k, base):
        lo = (k + reach_dev) * per_dev - base
        return tuple(x[lo : lo + per_dev] for x in part)

    parts = [fresh_part]
    for k in offsets:
        own_k = block_of(own_part, k, 0)
        if k >= 0:
            own_k = merge_all([own_k, block_of(prompt_part, k, start)])
        if k == 0:
            parts.append(own_k)
        else:
            parts.append(unpack(shifted(pack(own_k), "req", -k), shape4))
    weighted, _, totals = merge_all(parts)
    attended = (
        (weighted / totals[..., None])
        .reshape(per_dev, q_heads_local * head_dim)
        .astype(jnp.bfloat16)
    )
    partial_term = jnp.dot(attended, out_weight, preferred_element_type=jnp.float32)

    tp_count = lax.axis_size("tp")
    tp_index = lax.axis_index("tp")
    width = partial_term.shape[1] // tp_count
    total = lax.dynamic_slice_in_dim(partial_term, tp_index * width, width, axis=1)
    for step in range(1, tp_count):
        dest = (tp_index + step) % tp_count
        chunk = lax.dynamic_slice_in_dim(partial_term, dest * width, width, axis=1)
        route = [(i, (i + step) % tp_count) for i in range(tp_count)]
        got = lax.ppermute(chunk.astype(jnp.bfloat16), "tp", route)
        total = total + got.astype(jnp.float32)
    return total.astype(jnp.bfloat16)


def solution(mesh):
    in_specs = (
        P("req", "tp"),
        P("req", None, "tp"),
        P("req", None, None, "tp"),
        P("req", None, None, "tp"),
        P("tp", None),
        P(),
        P(),
        P(),
    )
    out_specs = P("req", "tp")
    return jax.shard_map(local, mesh=mesh, in_specs=in_specs, out_specs=out_specs, check_vma=False)
```

```python
import jax
import jax.numpy as jnp
from jax import lax
from jax.sharding import PartitionSpec as P

HD = 128
MOST_BEAMS = 16


MASKED_SCORE = -1e30


def shifted(block, axis, distance):
    devices = range(lax.axis_size(axis))
    route = [(i + distance, i) for i in devices if i + distance in devices]
    return lax.ppermute(block, axis, route)


def split_weights(weights):
    high = weights.astype(jnp.bfloat16)
    low = (weights - high.astype(jnp.float32)).astype(jnp.bfloat16)
    return high, low


def partial_block(query_block, key_block, value_block, allowed):
    score_scale = query_block.shape[-1] ** (-0.5)
    scores = jnp.einsum(
        "nkgd,skd->nkgs", query_block, key_block, preferred_element_type=jnp.float32
    )
    scores = scores * score_scale
    masked = allowed[:, None, None, :]
    scores = jnp.where(masked, scores, MASKED_SCORE)
    peaks = jnp.max(scores, axis=-1)
    weights = jnp.where(masked, jnp.exp(scores - peaks[..., None]), 0.0)
    totals = jnp.sum(weights, axis=-1)
    high, low = split_weights(weights)
    formula = "nkgs,skd->nkgd"
    weighted = jnp.einsum(
        formula, high, value_block, preferred_element_type=jnp.float32
    ) + jnp.einsum(formula, low, value_block, preferred_element_type=jnp.float32)
    return (weighted, peaks, totals)


def merge_all(parts):
    peaks = [jnp.where(p[2] > 0, p[1], MASKED_SCORE) for p in parts]
    top = peaks[0]
    for pk in peaks[1:]:
        top = jnp.maximum(top, pk)
    weighted = 0.0
    totals = 0.0
    for part, pk in zip(parts, peaks):
        scale = jnp.where(part[2] > 0, jnp.exp(pk - top), 0.0)
        weighted = weighted + part[0] * scale[..., None]
        totals = totals + part[2] * scale
    return (weighted, top, totals)


def pack(part):
    weighted, peaks, totals = part
    n = weighted.shape[0]
    return jnp.concatenate(
        [weighted.reshape(n, -1), peaks.reshape(n, -1), totals.reshape(n, -1)], axis=1
    )


def unpack(packed, shape):
    n, k, g, d = shape
    width = k * g * d
    weighted = packed[:, :width].reshape(n, k, g, d)
    peaks = packed[:, width : width + k * g].reshape(n, k, g)
    totals = packed[:, width + k * g :].reshape(n, k, g)
    return (weighted, peaks, totals)


def local(queries, new_kv, own_kv, prompt_kv, out_weight, parents, own_len, first_beam):
    per_dev = queries.shape[0]
    head_dim = HD
    kv_heads_local = new_kv.shape[2] // head_dim
    q_heads_local = queries.shape[1] // head_dim
    group_size = q_heads_local // kv_heads_local
    own_size = own_kv.shape[1]
    prompt_size = prompt_kv.shape[1]
    req_count = lax.axis_size("req")
    beam_count = per_dev * req_count
    dev_index = lax.axis_index("req")
    reach_dev = (MOST_BEAMS - 2) // per_dev + 1
    offsets = list(range(-reach_dev, reach_dev + 1))
    shape4 = (per_dev, kv_heads_local, group_size, head_dim)

    query_block = queries.reshape(shape4)
    hood = [query_block if k == 0 else shifted(query_block, "req", k) for k in offsets]
    hood_queries = jnp.concatenate(hood, axis=0)
    hood_count = hood_queries.shape[0]
    hood_beams = (dev_index - reach_dev) * per_dev + jnp.arange(hood_count, dtype=jnp.int32)
    in_range = (hood_beams >= 0) & (hood_beams < beam_count)
    clipped = jnp.clip(hood_beams, 0, beam_count - 1)

    parent = parents[clipped]
    lengths = own_len[parent]
    parent_here = in_range & (parent // per_dev == dev_index)
    columns = jnp.arange(per_dev * own_size, dtype=jnp.int32)
    own_allowed = (
        parent_here[:, None]
        & (columns[None, :] // own_size == (parent % per_dev)[:, None])
        & (columns[None, :] % own_size < lengths[:, None])
    )
    own_keys = own_kv[:, :, 0].reshape(per_dev * own_size, kv_heads_local, head_dim)
    own_values = own_kv[:, :, 1].reshape(per_dev * own_size, kv_heads_local, head_dim)
    own_part = partial_block(hood_queries, own_keys, own_values, own_allowed)

    start = reach_dev * per_dev
    home_here = in_range[start:] & (first_beam[clipped[start:]] // per_dev == dev_index)
    prompt_allowed = jnp.broadcast_to(home_here[:, None], (hood_count - start, prompt_size))
    prompt_keys = prompt_kv[0, :, 0].reshape(prompt_size, kv_heads_local, head_dim)
    prompt_values = prompt_kv[0, :, 1].reshape(prompt_size, kv_heads_local, head_dim)
    prompt_part = partial_block(hood_queries[start:], prompt_keys, prompt_values, prompt_allowed)

    fresh_keys = new_kv[:, 0].reshape(per_dev, 1, kv_heads_local, head_dim)
    fresh_values = new_kv[:, 1].reshape(per_dev, 1, kv_heads_local, head_dim)
    fresh_scores = jnp.einsum(
        "nkgd,nskd->nkgs", query_block, fresh_keys, preferred_element_type=jnp.float32
    ) * (head_dim ** (-0.5))
    fresh_part = (
        fresh_values[:, 0, :, None, :].astype(jnp.float32) * jnp.ones_like(fresh_scores),
        fresh_scores[..., 0],
        jnp.ones_like(fresh_scores[..., 0]),
    )

    def block_of(part, k, base):
        lo = (k + reach_dev) * per_dev - base
        return tuple(x[lo : lo + per_dev] for x in part)

    parts = [fresh_part]
    for k in offsets:
        own_k = block_of(own_part, k, 0)
        if k >= 0:
            own_k = merge_all([own_k, block_of(prompt_part, k, start)])
        if k == 0:
            parts.append(own_k)
        else:
            parts.append(unpack(shifted(pack(own_k), "req", -k), shape4))
    weighted, _, totals = merge_all(parts)
    attended = (
        (weighted / totals[..., None])
        .reshape(per_dev, q_heads_local * head_dim)
        .astype(jnp.bfloat16)
    )
    partial_term = jnp.dot(attended, out_weight, preferred_element_type=jnp.float32)

    tp_count = lax.axis_size("tp")
    tp_index = lax.axis_index("tp")
    width = partial_term.shape[1] // tp_count
    chunks = partial_term.reshape(per_dev, tp_count, width).transpose(1, 0, 2)
    got = lax.all_to_all(chunks.astype(jnp.bfloat16), "tp", 0, 0, tiled=True)
    others = jnp.arange(tp_count, dtype=jnp.int32)[:, None, None] != tp_index
    mine = lax.dynamic_slice_in_dim(partial_term, tp_index * width, width, axis=1)
    total = mine + jnp.sum(jnp.where(others, got.astype(jnp.float32), 0.0), axis=0)
    return total.astype(jnp.bfloat16)


def solution(mesh):
    in_specs = (
        P("req", "tp"),
        P("req", None, "tp"),
        P("req", None, None, "tp"),
        P("req", None, None, "tp"),
        P("tp", None),
        P(),
        P(),
        P(),
    )
    out_specs = P("req", "tp")
    return jax.shard_map(local, mesh=mesh, in_specs=in_specs, out_specs=out_specs, check_vma=False)
```

```python
import jax
import jax.numpy as jnp
from jax import lax
from jax.sharding import PartitionSpec as P

HD = 128
MOST_BEAMS = 16


MASKED_SCORE = -1e30


def shifted(block, axis, distance):
    devices = range(lax.axis_size(axis))
    route = [(i + distance, i) for i in devices if i + distance in devices]
    return lax.ppermute(block, axis, route)


def split_weights(weights):
    high = weights.astype(jnp.bfloat16)
    low = (weights - high.astype(jnp.float32)).astype(jnp.bfloat16)
    return high, low


def partial_block(query_block, key_block, value_block, allowed):
    score_scale = query_block.shape[-1] ** (-0.5)
    scores = jnp.einsum(
        "nkgd,skd->nkgs", query_block, key_block, preferred_element_type=jnp.float32
    )
    scores = scores * score_scale
    masked = allowed[:, None, None, :]
    scores = jnp.where(masked, scores, MASKED_SCORE)
    peaks = jnp.max(scores, axis=-1)
    weights = jnp.where(masked, jnp.exp(scores - peaks[..., None]), 0.0)
    totals = jnp.sum(weights, axis=-1)
    high, low = split_weights(weights)
    formula = "nkgs,skd->nkgd"
    weighted = jnp.einsum(
        formula, high, value_block, preferred_element_type=jnp.float32
    ) + jnp.einsum(formula, low, value_block, preferred_element_type=jnp.float32)
    return (weighted, peaks, totals)


def merge_all(parts):
    peaks = [jnp.where(p[2] > 0, p[1], MASKED_SCORE) for p in parts]
    top = peaks[0]
    for pk in peaks[1:]:
        top = jnp.maximum(top, pk)
    weighted = 0.0
    totals = 0.0
    for part, pk in zip(parts, peaks):
        scale = jnp.where(part[2] > 0, jnp.exp(pk - top), 0.0)
        weighted = weighted + part[0] * scale[..., None]
        totals = totals + part[2] * scale
    return (weighted, top, totals)


def pack(part):
    weighted, peaks, totals = part
    n = weighted.shape[0]
    return jnp.concatenate(
        [weighted.reshape(n, -1), peaks.reshape(n, -1), totals.reshape(n, -1)], axis=1
    )


def unpack(packed, shape):
    n, k, g, d = shape
    width = k * g * d
    weighted = packed[:, :width].reshape(n, k, g, d)
    peaks = packed[:, width : width + k * g].reshape(n, k, g)
    totals = packed[:, width + k * g :].reshape(n, k, g)
    return (weighted, peaks, totals)


def swapped(block, axis):
    devices = range(lax.axis_size(axis))
    return lax.ppermute(block, axis, [(i, i ^ 1) for i in devices])


def local(queries, new_kv, own_kv, prompt_kv, out_weight, parents, own_len, first_beam):
    per_dev = queries.shape[0]
    head_dim = HD
    kv_heads_local = new_kv.shape[2] // head_dim
    q_heads_local = queries.shape[1] // head_dim
    group_size = q_heads_local // kv_heads_local
    own_size = own_kv.shape[1]
    prompt_size = prompt_kv.shape[1]
    req_count = lax.axis_size("req")
    beam_count = per_dev * req_count
    dev_index = lax.axis_index("req")
    core = dev_index % 2
    first_core = core == 0
    chip_beams = 2 * per_dev
    shape4 = (per_dev, kv_heads_local, group_size, head_dim)

    query_block = queries.reshape(shape4)
    from_prev = shifted(query_block, "req", -2)
    from_next = shifted(query_block, "req", 2)
    mine3 = jnp.concatenate([from_prev, query_block, from_next], axis=0)
    mate3 = swapped(mine3, "req")
    hood = []
    for i in range(3):
        a = mine3[i * per_dev : (i + 1) * per_dev]
        b = mate3[i * per_dev : (i + 1) * per_dev]
        hood += [jnp.where(first_core, a, b), jnp.where(first_core, b, a)]
    hood_queries = jnp.concatenate(hood, axis=0)
    hood_count = hood_queries.shape[0]
    chip = dev_index // 2
    hood_start = (chip - 1) * chip_beams
    hood_beams = hood_start + jnp.arange(hood_count, dtype=jnp.int32)
    in_range = (hood_beams >= 0) & (hood_beams < beam_count)
    padded_parents = jnp.pad(parents, (chip_beams, chip_beams))
    padded_first = jnp.pad(first_beam, (chip_beams, chip_beams))
    parent = lax.dynamic_slice_in_dim(padded_parents, chip * chip_beams, hood_count)
    hood_first = lax.dynamic_slice_in_dim(padded_first, chip * chip_beams, hood_count)

    parent_here = in_range & (parent // per_dev == dev_index)
    local_len = lax.dynamic_slice_in_dim(own_len, dev_index * per_dev, per_dev)
    columns = jnp.arange(per_dev * own_size, dtype=jnp.int32)
    column_slot = columns // own_size
    column_len = jnp.repeat(local_len, own_size)
    own_allowed = (
        parent_here[:, None]
        & (column_slot[None, :] == (parent % per_dev)[:, None])
        & (columns % own_size < column_len)[None, :]
    )
    own_keys = own_kv[:, :, 0].reshape(per_dev * own_size, kv_heads_local, head_dim)
    own_values = own_kv[:, :, 1].reshape(per_dev * own_size, kv_heads_local, head_dim)
    own_part = partial_block(hood_queries, own_keys, own_values, own_allowed)

    start = chip_beams
    home_here = in_range[start:] & (hood_first[start:] // per_dev == dev_index)
    prompt_allowed = jnp.broadcast_to(home_here[:, None], (hood_count - start, prompt_size))
    prompt_keys = prompt_kv[0, :, 0].reshape(prompt_size, kv_heads_local, head_dim)
    prompt_values = prompt_kv[0, :, 1].reshape(prompt_size, kv_heads_local, head_dim)
    prompt_part = partial_block(hood_queries[start:], prompt_keys, prompt_values, prompt_allowed)

    fresh_keys = new_kv[:, 0].reshape(per_dev, 1, kv_heads_local, head_dim)
    fresh_values = new_kv[:, 1].reshape(per_dev, 1, kv_heads_local, head_dim)
    fresh_scores = jnp.einsum(
        "nkgd,nskd->nkgs", query_block, fresh_keys, preferred_element_type=jnp.float32
    ) * (head_dim ** (-0.5))
    fresh_part = (
        fresh_values[:, 0, :, None, :].astype(jnp.float32) * jnp.ones_like(fresh_scores),
        fresh_scores[..., 0],
        jnp.ones_like(fresh_scores[..., 0]),
    )

    def rows(part, lo):
        return tuple(x[lo : lo + per_dev] for x in part)

    def block_for(chip_offset, which_core):
        lo = (chip_offset + 1) * chip_beams + which_core * per_dev
        own_k = rows(own_part, lo)
        if chip_offset >= 0:
            return merge_all([own_k, rows(prompt_part, lo - start)])
        return own_k

    def pick(which_first, which_second):
        return tuple(jnp.where(first_core, a, b) for a, b in zip(which_first, which_second))

    mate_core = 1 - core
    to_mate = [
        pick(block_for(k, 1), block_for(k, 0)) for k in (-1, 0, 1)
    ]
    mine_blocks = [
        pick(block_for(k, 0), block_for(k, 1)) for k in (-1, 0, 1)
    ]
    del mate_core
    sent = swapped(jnp.concatenate([pack(b) for b in to_mate], axis=0), "req")
    got = [unpack(sent[i * per_dev : (i + 1) * per_dev], shape4) for i in range(3)]
    merged = [merge_all([mine_blocks[i], got[i]]) for i in range(3)]
    back_from_next = unpack(shifted(pack(merged[0]), "req", 2), shape4)
    back_from_prev = unpack(shifted(pack(merged[2]), "req", -2), shape4)
    weighted, _, totals = merge_all([fresh_part, merged[1], back_from_next, back_from_prev])
    attended = (
        (weighted / totals[..., None])
        .reshape(per_dev, q_heads_local * head_dim)
        .astype(jnp.bfloat16)
    )
    partial_term = jnp.dot(attended, out_weight, preferred_element_type=jnp.float32)

    tp_count = lax.axis_size("tp")
    tp_index = lax.axis_index("tp")
    width = partial_term.shape[1] // tp_count
    chunks = partial_term.reshape(per_dev, tp_count, width).transpose(1, 0, 2)
    got = lax.all_to_all(chunks.astype(jnp.bfloat16), "tp", 0, 0, tiled=True)
    others = jnp.arange(tp_count, dtype=jnp.int32)[:, None, None] != tp_index
    mine = lax.dynamic_slice_in_dim(partial_term, tp_index * width, width, axis=1)
    total = mine + jnp.sum(jnp.where(others, got.astype(jnp.float32), 0.0), axis=0)
    return total.astype(jnp.bfloat16)


def solution(mesh):
    in_specs = (
        P("req", "tp"),
        P("req", None, "tp"),
        P("req", None, None, "tp"),
        P("req", None, None, "tp"),
        P("tp", None),
        P(),
        P(),
        P(),
    )
    out_specs = P("req", "tp")
    return jax.shard_map(local, mesh=mesh, in_specs=in_specs, out_specs=out_specs, check_vma=False)
```

```python
import jax
import jax.numpy as jnp
from jax import lax
from jax.experimental import pallas as pl
from jax.sharding import PartitionSpec as P

HD = 128
MOST_BEAMS = 16


MASKED_SCORE = -1e30


def shifted(block, axis, distance):
    devices = range(lax.axis_size(axis))
    route = [(i + distance, i) for i in devices if i + distance in devices]
    return lax.ppermute(block, axis, route)


def split_weights(weights):
    high = weights.astype(jnp.bfloat16)
    low = (weights - high.astype(jnp.float32)).astype(jnp.bfloat16)
    return high, low


def partial_block(query_block, key_block, value_block, allowed):
    score_scale = query_block.shape[-1] ** (-0.5)
    scores = jnp.einsum(
        "nkgd,skd->nkgs", query_block, key_block, preferred_element_type=jnp.float32
    )
    scores = scores * score_scale
    masked = allowed[:, None, None, :]
    scores = jnp.where(masked, scores, MASKED_SCORE)
    peaks = jnp.max(scores, axis=-1)
    weights = jnp.where(masked, jnp.exp(scores - peaks[..., None]), 0.0)
    totals = jnp.sum(weights, axis=-1)
    high, low = split_weights(weights)
    formula = "nkgs,skd->nkgd"
    weighted = jnp.einsum(
        formula, high, value_block, preferred_element_type=jnp.float32
    ) + jnp.einsum(formula, low, value_block, preferred_element_type=jnp.float32)
    return (weighted, peaks, totals)


def merge_all(parts):
    peaks = [jnp.where(p[2] > 0, p[1], MASKED_SCORE) for p in parts]
    top = peaks[0]
    for pk in peaks[1:]:
        top = jnp.maximum(top, pk)
    weighted = 0.0
    totals = 0.0
    for part, pk in zip(parts, peaks):
        scale = jnp.where(part[2] > 0, jnp.exp(pk - top), 0.0)
        weighted = weighted + part[0] * scale[..., None]
        totals = totals + part[2] * scale
    return (weighted, top, totals)


def pack(part):
    weighted, peaks, totals = part
    n = weighted.shape[0]
    return jnp.concatenate(
        [weighted.reshape(n, -1), peaks.reshape(n, -1), totals.reshape(n, -1)], axis=1
    )


def unpack(packed, shape):
    n, k, g, d = shape
    width = k * g * d
    weighted = packed[:, :width].reshape(n, k, g, d)
    peaks = packed[:, width : width + k * g].reshape(n, k, g)
    totals = packed[:, width + k * g :].reshape(n, k, g)
    return (weighted, peaks, totals)


def project_kernel(x_ref, w_ref, o_ref):
    o_ref[0] = jnp.dot(x_ref[...], w_ref[...], preferred_element_type=jnp.float32)


def project(attended, weight, pieces):
    n, inner = attended.shape
    width = weight.shape[1] // pieces
    return pl.pallas_call(
        project_kernel,
        grid=(pieces,),
        in_specs=[
            pl.BlockSpec((n, inner), lambda j: (0, 0)),
            pl.BlockSpec((inner, width), lambda j: (0, j)),
        ],
        out_specs=pl.BlockSpec((1, n, width), lambda j: (j, 0, 0)),
        out_shape=jax.ShapeDtypeStruct((pieces, n, width), jnp.float32),
    )(attended, weight)


def swapped(block, axis):
    devices = range(lax.axis_size(axis))
    return lax.ppermute(block, axis, [(i, i ^ 1) for i in devices])


def local(queries, new_kv, own_kv, prompt_kv, out_weight, parents, own_len, first_beam):
    per_dev = queries.shape[0]
    head_dim = HD
    kv_heads_local = new_kv.shape[2] // head_dim
    q_heads_local = queries.shape[1] // head_dim
    group_size = q_heads_local // kv_heads_local
    own_size = own_kv.shape[1]
    prompt_size = prompt_kv.shape[1]
    req_count = lax.axis_size("req")
    beam_count = per_dev * req_count
    dev_index = lax.axis_index("req")
    core = dev_index % 2
    first_core = core == 0
    chip_beams = 2 * per_dev
    shape4 = (per_dev, kv_heads_local, group_size, head_dim)

    query_block = queries.reshape(shape4)
    from_prev = shifted(queries, "req", -2)
    from_next = shifted(queries, "req", 2)
    mine3 = jnp.concatenate([from_prev, queries, from_next], axis=0)
    mate3 = swapped(mine3, "req")
    mine3 = mine3.reshape((3 * per_dev,) + shape4[1:])
    mate3 = mate3.reshape((3 * per_dev,) + shape4[1:])
    hood = []
    for i in range(3):
        a = mine3[i * per_dev : (i + 1) * per_dev]
        b = mate3[i * per_dev : (i + 1) * per_dev]
        hood += [jnp.where(first_core, a, b), jnp.where(first_core, b, a)]
    hood_queries = jnp.concatenate(hood, axis=0)
    hood_count = hood_queries.shape[0]
    chip = dev_index // 2
    hood_start = (chip - 1) * chip_beams
    hood_beams = hood_start + jnp.arange(hood_count, dtype=jnp.int32)
    in_range = (hood_beams >= 0) & (hood_beams < beam_count)
    index_rows = jnp.pad(
        jnp.stack([parents, first_beam, own_len]), ((0, 0), (chip_beams, chip_beams))
    )
    window = lax.dynamic_slice_in_dim(index_rows, chip * chip_beams, hood_count, axis=1)
    parent = window[0]
    hood_first = window[1]

    parent_here = in_range & (parent // per_dev == dev_index)
    local_len = lax.dynamic_slice_in_dim(window[2], chip_beams + core * per_dev, per_dev)
    columns = jnp.arange(per_dev * own_size, dtype=jnp.int32)
    column_slot = columns // own_size
    column_len = jnp.repeat(local_len, own_size)
    own_allowed = (
        parent_here[:, None]
        & (column_slot[None, :] == (parent % per_dev)[:, None])
        & (columns % own_size < column_len)[None, :]
    )
    own_split = jnp.moveaxis(own_kv.reshape(per_dev * own_size, 2, -1), 1, 0)
    own_keys = own_split[0].reshape(per_dev * own_size, kv_heads_local, head_dim)
    own_values = own_split[1].reshape(per_dev * own_size, kv_heads_local, head_dim)
    own_part = partial_block(hood_queries, own_keys, own_values, own_allowed)

    start = chip_beams
    home_here = in_range[start:] & (hood_first[start:] // per_dev == dev_index)
    prompt_allowed = jnp.broadcast_to(home_here[:, None], (hood_count - start, prompt_size))
    prompt_split = jnp.moveaxis(prompt_kv[0], 1, 0)
    prompt_keys = prompt_split[0].reshape(prompt_size, kv_heads_local, head_dim)
    prompt_values = prompt_split[1].reshape(prompt_size, kv_heads_local, head_dim)
    prompt_part = partial_block(hood_queries[start:], prompt_keys, prompt_values, prompt_allowed)

    fresh_keys = new_kv[:, 0].reshape(per_dev, 1, kv_heads_local, head_dim)
    fresh_values = new_kv[:, 1].reshape(per_dev, 1, kv_heads_local, head_dim)
    fresh_scores = jnp.einsum(
        "nkgd,nskd->nkgs", query_block, fresh_keys, preferred_element_type=jnp.float32
    ) * (head_dim ** (-0.5))
    fresh_part = (
        fresh_values[:, 0, :, None, :].astype(jnp.float32) * jnp.ones_like(fresh_scores),
        fresh_scores[..., 0],
        jnp.ones_like(fresh_scores[..., 0]),
    )

    def rows(part, lo):
        return tuple(x[lo : lo + per_dev] for x in part)

    def block_for(chip_offset, which_core):
        lo = (chip_offset + 1) * chip_beams + which_core * per_dev
        own_k = rows(own_part, lo)
        if chip_offset >= 0:
            return merge_all([own_k, rows(prompt_part, lo - start)])
        return own_k

    def pick(which_first, which_second):
        return tuple(jnp.where(first_core, a, b) for a, b in zip(which_first, which_second))

    mate_core = 1 - core
    to_mate = [
        pick(block_for(k, 1), block_for(k, 0)) for k in (-1, 0, 1)
    ]
    mine_blocks = [
        pick(block_for(k, 0), block_for(k, 1)) for k in (-1, 0, 1)
    ]
    del mate_core
    sent = swapped(jnp.concatenate([pack(b) for b in to_mate], axis=0), "req")
    got = [unpack(sent[i * per_dev : (i + 1) * per_dev], shape4) for i in range(3)]
    merged = [merge_all([mine_blocks[i], got[i]]) for i in range(3)]
    back_from_next = unpack(shifted(pack(merged[0]), "req", 2), shape4)
    back_from_prev = unpack(shifted(pack(merged[2]), "req", -2), shape4)
    weighted, _, totals = merge_all([fresh_part, merged[1], back_from_next, back_from_prev])
    attended = (
        (weighted / totals[..., None])
        .reshape(per_dev, q_heads_local * head_dim)
        .astype(jnp.bfloat16)
    )
    tp_count = lax.axis_size("tp")
    tp_index = lax.axis_index("tp")
    chunks = project(attended, out_weight, tp_count)

    got = lax.all_to_all(chunks.astype(jnp.bfloat16), "tp", 0, 0, tiled=True)
    others = jnp.arange(tp_count, dtype=jnp.int32)[:, None, None] != tp_index
    mine = lax.dynamic_index_in_dim(chunks, tp_index, axis=0, keepdims=False)
    total = mine + jnp.sum(jnp.where(others, got.astype(jnp.float32), 0.0), axis=0)
    return total.astype(jnp.bfloat16)


def solution(mesh):
    in_specs = (
        P("req", "tp"),
        P("req", None, "tp"),
        P("req", None, None, "tp"),
        P("req", None, None, "tp"),
        P("tp", None),
        P(),
        P(),
        P(),
    )
    out_specs = P("req", "tp")
    return jax.shard_map(local, mesh=mesh, in_specs=in_specs, out_specs=out_specs, check_vma=False)
```

```python
import jax
import jax.numpy as jnp
from jax import lax
from jax.sharding import PartitionSpec as P

HD = 128
MOST_BEAMS = 16


MASKED_SCORE = -1e30


def shifted(block, axis, distance):
    devices = range(lax.axis_size(axis))
    route = [(i + distance, i) for i in devices if i + distance in devices]
    return lax.ppermute(block, axis, route)


def split_weights(weights):
    high = weights.astype(jnp.bfloat16)
    low = (weights - high.astype(jnp.float32)).astype(jnp.bfloat16)
    return high, low


def partial_block(query_block, key_block, value_block, allowed):
    score_scale = query_block.shape[-1] ** (-0.5)
    scores = jnp.einsum(
        "nkgd,skd->nkgs", query_block, key_block, preferred_element_type=jnp.float32
    )
    scores = scores * score_scale
    masked = allowed[:, None, None, :]
    scores = jnp.where(masked, scores, MASKED_SCORE)
    peaks = jnp.max(scores, axis=-1)
    weights = jnp.where(masked, jnp.exp(scores - peaks[..., None]), 0.0)
    totals = jnp.sum(weights, axis=-1)
    high, low = split_weights(weights)
    formula = "nkgs,skd->nkgd"
    weighted = jnp.einsum(
        formula, high, value_block, preferred_element_type=jnp.float32
    ) + jnp.einsum(formula, low, value_block, preferred_element_type=jnp.float32)
    return (weighted, peaks, totals)


def merge_all(parts):
    peaks = [jnp.where(p[2] > 0, p[1], MASKED_SCORE) for p in parts]
    top = peaks[0]
    for pk in peaks[1:]:
        top = jnp.maximum(top, pk)
    weighted = 0.0
    totals = 0.0
    for part, pk in zip(parts, peaks):
        scale = jnp.where(part[2] > 0, jnp.exp(pk - top), 0.0)
        weighted = weighted + part[0] * scale[..., None]
        totals = totals + part[2] * scale
    return (weighted, top, totals)


def pack(part):
    weighted, peaks, totals = part
    n = weighted.shape[0]
    return jnp.concatenate(
        [weighted.reshape(n, -1), peaks.reshape(n, -1), totals.reshape(n, -1)], axis=1
    )


def unpack(packed, shape):
    n, k, g, d = shape
    width = k * g * d
    weighted = packed[:, :width].reshape(n, k, g, d)
    peaks = packed[:, width : width + k * g].reshape(n, k, g)
    totals = packed[:, width + k * g :].reshape(n, k, g)
    return (weighted, peaks, totals)


def swapped(block, axis):
    devices = range(lax.axis_size(axis))
    return lax.ppermute(block, axis, [(i, i ^ 1) for i in devices])


def local(queries, new_kv, own_kv, prompt_kv, out_weight, parents, own_len, first_beam):
    per_dev = queries.shape[0]
    head_dim = HD
    kv_heads_local = new_kv.shape[2] // head_dim
    q_heads_local = queries.shape[1] // head_dim
    group_size = q_heads_local // kv_heads_local
    own_size = own_kv.shape[1]
    prompt_size = prompt_kv.shape[1]
    req_count = lax.axis_size("req")
    beam_count = per_dev * req_count
    dev_index = lax.axis_index("req")
    core = dev_index % 2
    first_core = core == 0
    chip_beams = 2 * per_dev
    shape4 = (per_dev, kv_heads_local, group_size, head_dim)

    query_block = queries.reshape(shape4)
    from_prev = shifted(queries, "req", -2)
    from_next = shifted(queries, "req", 2)
    mine3 = jnp.concatenate([from_prev, queries, from_next], axis=0)
    mate3 = swapped(mine3, "req")
    mine3 = mine3.reshape((3 * per_dev,) + shape4[1:])
    mate3 = mate3.reshape((3 * per_dev,) + shape4[1:])
    hood = []
    for i in range(3):
        a = mine3[i * per_dev : (i + 1) * per_dev]
        b = mate3[i * per_dev : (i + 1) * per_dev]
        hood += [jnp.where(first_core, a, b), jnp.where(first_core, b, a)]
    hood_queries = jnp.concatenate(hood, axis=0)
    hood_count = hood_queries.shape[0]
    chip = dev_index // 2
    hood_start = (chip - 1) * chip_beams
    hood_beams = hood_start + jnp.arange(hood_count, dtype=jnp.int32)
    in_range = (hood_beams >= 0) & (hood_beams < beam_count)
    index_rows = jnp.pad(
        jnp.stack([parents, first_beam, own_len]), ((0, 0), (chip_beams, chip_beams))
    )
    window = lax.dynamic_slice_in_dim(index_rows, chip * chip_beams, hood_count, axis=1)
    parent = window[0]
    hood_first = window[1]

    parent_here = in_range & (parent // per_dev == dev_index)
    local_len = lax.dynamic_slice_in_dim(window[2], chip_beams + core * per_dev, per_dev)
    columns = jnp.arange(per_dev * own_size, dtype=jnp.int32)
    column_slot = columns // own_size
    column_len = jnp.repeat(local_len, own_size)
    own_allowed = (
        parent_here[:, None]
        & (column_slot[None, :] == (parent % per_dev)[:, None])
        & (columns % own_size < column_len)[None, :]
    )
    own_split = jnp.moveaxis(own_kv.reshape(per_dev * own_size, 2, -1), 1, 0)
    own_keys = own_split[0].reshape(per_dev * own_size, kv_heads_local, head_dim)
    own_values = own_split[1].reshape(per_dev * own_size, kv_heads_local, head_dim)
    own_part = partial_block(hood_queries, own_keys, own_values, own_allowed)

    start = chip_beams
    home_here = in_range[start:] & (hood_first[start:] // per_dev == dev_index)
    prompt_allowed = jnp.broadcast_to(home_here[:, None], (hood_count - start, prompt_size))
    prompt_split = jnp.moveaxis(prompt_kv[0], 1, 0)
    prompt_keys = prompt_split[0].reshape(prompt_size, kv_heads_local, head_dim)
    prompt_values = prompt_split[1].reshape(prompt_size, kv_heads_local, head_dim)
    prompt_part = partial_block(hood_queries[start:], prompt_keys, prompt_values, prompt_allowed)

    fresh_keys = new_kv[:, 0].reshape(per_dev, 1, kv_heads_local, head_dim)
    fresh_values = new_kv[:, 1].reshape(per_dev, 1, kv_heads_local, head_dim)
    fresh_scores = jnp.einsum(
        "nkgd,nskd->nkgs", query_block, fresh_keys, preferred_element_type=jnp.float32
    ) * (head_dim ** (-0.5))
    fresh_part = (
        fresh_values[:, 0, :, None, :].astype(jnp.float32) * jnp.ones_like(fresh_scores),
        fresh_scores[..., 0],
        jnp.ones_like(fresh_scores[..., 0]),
    )

    def rows(part, lo):
        return tuple(x[lo : lo + per_dev] for x in part)

    def block_for(chip_offset, which_core):
        lo = (chip_offset + 1) * chip_beams + which_core * per_dev
        own_k = rows(own_part, lo)
        if chip_offset >= 0:
            return merge_all([own_k, rows(prompt_part, lo - start)])
        return own_k

    def pick(which_first, which_second):
        return tuple(jnp.where(first_core, a, b) for a, b in zip(which_first, which_second))

    mate_core = 1 - core
    to_mate = [
        pick(block_for(k, 1), block_for(k, 0)) for k in (-1, 0, 1)
    ]
    mine_blocks = [
        pick(block_for(k, 0), block_for(k, 1)) for k in (-1, 0, 1)
    ]
    del mate_core
    sent = swapped(jnp.concatenate([pack(b) for b in to_mate], axis=0), "req")
    got = [unpack(sent[i * per_dev : (i + 1) * per_dev], shape4) for i in range(3)]
    merged = [merge_all([mine_blocks[i], got[i]]) for i in range(3)]
    back_from_next = unpack(shifted(pack(merged[0]), "req", 2), shape4)
    back_from_prev = unpack(shifted(pack(merged[2]), "req", -2), shape4)
    weighted, _, totals = merge_all([fresh_part, merged[1], back_from_next, back_from_prev])
    attended = (
        (weighted / totals[..., None])
        .reshape(per_dev, q_heads_local * head_dim)
        .astype(jnp.bfloat16)
    )
    partial_term = jnp.dot(attended, out_weight, preferred_element_type=jnp.float32)

    tp_count = lax.axis_size("tp")
    tp_index = lax.axis_index("tp")
    kept = partial_term
    span = partial_term.shape[1]
    distance = tp_count // 2
    while distance >= 1:
        span //= 2
        side = (tp_index // distance) % 2
        mine = lax.dynamic_slice_in_dim(kept, side * span, span, axis=1)
        other = lax.dynamic_slice_in_dim(kept, (1 - side) * span, span, axis=1)
        route = [(i, i ^ distance) for i in range(tp_count)]
        got = lax.ppermute(other.astype(jnp.bfloat16), "tp", route)
        kept = mine + got.astype(jnp.float32)
        distance //= 2
    return kept.astype(jnp.bfloat16)


def solution(mesh):
    in_specs = (
        P("req", "tp"),
        P("req", None, "tp"),
        P("req", None, None, "tp"),
        P("req", None, None, "tp"),
        P("tp", None),
        P(),
        P(),
        P(),
    )
    out_specs = P("req", "tp")
    return jax.shard_map(local, mesh=mesh, in_specs=in_specs, out_specs=out_specs, check_vma=False)
```

```python
import jax
import jax.numpy as jnp
from jax import lax
from jax.sharding import PartitionSpec as P

HD = 128
MOST_BEAMS = 16


MASKED_SCORE = -1e30


def shifted(block, axis, distance):
    devices = range(lax.axis_size(axis))
    route = [(i + distance, i) for i in devices if i + distance in devices]
    return lax.ppermute(block, axis, route)


def split_weights(weights):
    high = weights.astype(jnp.bfloat16)
    low = (weights - high.astype(jnp.float32)).astype(jnp.bfloat16)
    return high, low


def partial_block(query_block, key_block, value_block, allowed):
    score_scale = query_block.shape[-1] ** (-0.5)
    scores = jnp.einsum(
        "nkgd,skd->nkgs", query_block, key_block, preferred_element_type=jnp.float32
    )
    scores = scores * score_scale
    masked = allowed[:, None, None, :]
    scores = jnp.where(masked, scores, MASKED_SCORE)
    peaks = jnp.max(scores, axis=-1)
    weights = jnp.where(masked, jnp.exp(scores - peaks[..., None]), 0.0)
    totals = jnp.sum(weights, axis=-1)
    high, low = split_weights(weights)
    formula = "nkgs,skd->nkgd"
    weighted = jnp.einsum(
        formula, high, value_block, preferred_element_type=jnp.float32
    ) + jnp.einsum(formula, low, value_block, preferred_element_type=jnp.float32)
    return (weighted, peaks, totals)


def merge_all(parts):
    peaks = [jnp.where(p[2] > 0, p[1], MASKED_SCORE) for p in parts]
    top = peaks[0]
    for pk in peaks[1:]:
        top = jnp.maximum(top, pk)
    weighted = 0.0
    totals = 0.0
    for part, pk in zip(parts, peaks):
        scale = jnp.where(part[2] > 0, jnp.exp(pk - top), 0.0)
        weighted = weighted + part[0] * scale[..., None]
        totals = totals + part[2] * scale
    return (weighted, top, totals)


def pack(part):
    weighted, peaks, totals = part
    n = weighted.shape[0]
    return jnp.concatenate(
        [weighted.reshape(n, -1), peaks.reshape(n, -1), totals.reshape(n, -1)], axis=1
    )


def unpack(packed, shape):
    n, k, g, d = shape
    width = k * g * d
    weighted = packed[:, :width].reshape(n, k, g, d)
    peaks = packed[:, width : width + k * g].reshape(n, k, g)
    totals = packed[:, width + k * g :].reshape(n, k, g)
    return (weighted, peaks, totals)


def swapped(block, axis):
    devices = range(lax.axis_size(axis))
    return lax.ppermute(block, axis, [(i, i ^ 1) for i in devices])


def local(queries, new_kv, own_kv, prompt_kv, out_weight, parents, own_len, first_beam):
    per_dev = queries.shape[0]
    head_dim = HD
    kv_heads_local = new_kv.shape[2] // head_dim
    q_heads_local = queries.shape[1] // head_dim
    group_size = q_heads_local // kv_heads_local
    own_size = own_kv.shape[1]
    prompt_size = prompt_kv.shape[1]
    req_count = lax.axis_size("req")
    beam_count = per_dev * req_count
    dev_index = lax.axis_index("req")
    mate_index = dev_index ^ 1
    chip = dev_index // 2
    shape4 = (per_dev, kv_heads_local, group_size, head_dim)
    cache_rows = per_dev * own_size

    local_rows = jnp.concatenate(
        [own_kv.reshape(cache_rows, 2, -1), prompt_kv[0]], axis=0
    )
    local_kv = jnp.moveaxis(local_rows, 1, 0)
    mate_kv = swapped(local_kv, "req")

    from_prev = shifted(queries, "req", -2)
    from_next = shifted(queries, "req", 2)
    hood_queries = jnp.concatenate([from_prev, queries, from_next], axis=0)
    hood_queries = hood_queries.reshape((3 * per_dev,) + shape4[1:])
    query_block = queries.reshape(shape4)
    hood_count = 3 * per_dev
    slot_ids = jnp.arange(per_dev, dtype=jnp.int32)
    hood_beams = jnp.concatenate(
        [(dev_index + k) * per_dev + slot_ids for k in (-2, 0, 2)]
    )
    in_range = (hood_beams >= 0) & (hood_beams < beam_count)
    pad = 2 * per_dev
    index_rows = jnp.pad(jnp.stack([parents, first_beam, own_len]), ((0, 0), (pad, pad)))
    window = lax.dynamic_slice_in_dim(index_rows, dev_index * per_dev, 5 * per_dev, axis=1)
    hood_index = jnp.concatenate(
        [window[:, 0:per_dev], window[:, 2 * per_dev : 3 * per_dev], window[:, 4 * per_dev :]],
        axis=1,
    )
    parent = hood_index[0]
    home = hood_index[1] // per_dev
    local_len = window[2, pad : pad + per_dev]
    mate_len = lax.dynamic_slice_in_dim(
        window[2], 3 * per_dev - 2 * per_dev * (dev_index % 2), per_dev
    )
    parent_dev = parent // per_dev
    columns = jnp.arange(cache_rows, dtype=jnp.int32)
    column_slot = columns // own_size

    def own_allowed(holder, lengths):
        return (
            (in_range & (parent_dev == holder))[:, None]
            & (column_slot[None, :] == (parent % per_dev)[:, None])
            & (columns % own_size < jnp.repeat(lengths, own_size))[None, :]
        )

    def kv_rows(kv, lo, count):
        keys = kv[0, lo : lo + count].reshape(count, kv_heads_local, head_dim)
        values = kv[1, lo : lo + count].reshape(count, kv_heads_local, head_dim)
        return keys, values

    start = per_dev
    prompt_queries = hood_queries[start:]

    def prompt_allowed(holder):
        here = in_range[start:] & (home[start:] == holder)
        return jnp.broadcast_to(here[:, None], (hood_count - start, prompt_size))

    parts_here = []
    for kv, holder, lengths in ((local_kv, dev_index, local_len), (mate_kv, mate_index, mate_len)):
        keys, values = kv_rows(kv, 0, cache_rows)
        own_part = partial_block(hood_queries, keys, values, own_allowed(holder, lengths))
        keys, values = kv_rows(kv, cache_rows, prompt_size)
        prompt_part = partial_block(prompt_queries, keys, values, prompt_allowed(holder))
        prompt_full = tuple(
            jnp.concatenate([jnp.zeros_like(x[:start]), x], axis=0) for x in prompt_part
        )
        parts_here += [own_part, prompt_full]
    hood_part = merge_all(parts_here)

    fresh_keys = new_kv[:, 0].reshape(per_dev, 1, kv_heads_local, head_dim)
    fresh_values = new_kv[:, 1].reshape(per_dev, 1, kv_heads_local, head_dim)
    fresh_scores = jnp.einsum(
        "nkgd,nskd->nkgs", query_block, fresh_keys, preferred_element_type=jnp.float32
    ) * (head_dim ** (-0.5))
    fresh_part = (
        fresh_values[:, 0, :, None, :].astype(jnp.float32) * jnp.ones_like(fresh_scores),
        fresh_scores[..., 0],
        jnp.ones_like(fresh_scores[..., 0]),
    )

    def rows(part, lo):
        return tuple(x[lo : lo + per_dev] for x in part)

    back_from_next = unpack(shifted(pack(rows(hood_part, 0)), "req", 2), shape4)
    back_from_prev = unpack(shifted(pack(rows(hood_part, 2 * per_dev)), "req", -2), shape4)
    weighted, _, totals = merge_all(
        [fresh_part, rows(hood_part, per_dev), back_from_next, back_from_prev]
    )
    attended = (
        (weighted / totals[..., None])
        .reshape(per_dev, q_heads_local * head_dim)
        .astype(jnp.bfloat16)
    )
    partial_term = jnp.dot(attended, out_weight, preferred_element_type=jnp.float32)

    tp_count = lax.axis_size("tp")
    tp_index = lax.axis_index("tp")
    kept = partial_term
    span = partial_term.shape[1]
    distance = tp_count // 2
    while distance >= 1:
        span //= 2
        side = (tp_index // distance) % 2
        mine = lax.dynamic_slice_in_dim(kept, side * span, span, axis=1)
        other = lax.dynamic_slice_in_dim(kept, (1 - side) * span, span, axis=1)
        route = [(i, i ^ distance) for i in range(tp_count)]
        got = lax.ppermute(other.astype(jnp.bfloat16), "tp", route)
        kept = mine + got.astype(jnp.float32)
        distance //= 2
    return kept.astype(jnp.bfloat16)


def solution(mesh):
    in_specs = (
        P("req", "tp"),
        P("req", None, "tp"),
        P("req", None, None, "tp"),
        P("req", None, None, "tp"),
        P("tp", None),
        P(),
        P(),
        P(),
    )
    out_specs = P("req", "tp")
    return jax.shard_map(local, mesh=mesh, in_specs=in_specs, out_specs=out_specs, check_vma=False)
```

```python
import jax
import jax.numpy as jnp
from jax import lax
from jax.sharding import PartitionSpec as P

HD = 128
MOST_BEAMS = 16


MASKED_SCORE = -1e30


def shifted(block, axis, distance):
    devices = range(lax.axis_size(axis))
    route = [(i + distance, i) for i in devices if i + distance in devices]
    return lax.ppermute(block, axis, route)


def split_weights(weights):
    high = weights.astype(jnp.bfloat16)
    low = (weights - high.astype(jnp.float32)).astype(jnp.bfloat16)
    return high, low


def partial_block(query_block, key_block, value_block, allowed):
    score_scale = query_block.shape[-1] ** (-0.5)
    scores = jnp.einsum(
        "nkgd,skd->nkgs", query_block, key_block, preferred_element_type=jnp.float32
    )
    scores = scores * score_scale
    masked = allowed[:, None, None, :]
    scores = jnp.where(masked, scores, MASKED_SCORE)
    peaks = jnp.max(scores, axis=-1)
    weights = jnp.where(masked, jnp.exp(scores - peaks[..., None]), 0.0)
    totals = jnp.sum(weights, axis=-1)
    high, low = split_weights(weights)
    formula = "nkgs,skd->nkgd"
    weighted = jnp.einsum(
        formula, high, value_block, preferred_element_type=jnp.float32
    ) + jnp.einsum(formula, low, value_block, preferred_element_type=jnp.float32)
    return (weighted, peaks, totals)


def merge_all(parts):
    peaks = [jnp.where(p[2] > 0, p[1], MASKED_SCORE) for p in parts]
    top = peaks[0]
    for pk in peaks[1:]:
        top = jnp.maximum(top, pk)
    weighted = 0.0
    totals = 0.0
    for part, pk in zip(parts, peaks):
        scale = jnp.where(part[2] > 0, jnp.exp(pk - top), 0.0)
        weighted = weighted + part[0] * scale[..., None]
        totals = totals + part[2] * scale
    return (weighted, top, totals)


def pack(part):
    weighted, peaks, totals = part
    n = weighted.shape[0]
    return jnp.concatenate(
        [weighted.reshape(n, -1), peaks.reshape(n, -1), totals.reshape(n, -1)], axis=1
    )


def unpack(packed, shape):
    n, k, g, d = shape
    width = k * g * d
    weighted = packed[:, :width].reshape(n, k, g, d)
    peaks = packed[:, width : width + k * g].reshape(n, k, g)
    totals = packed[:, width + k * g :].reshape(n, k, g)
    return (weighted, peaks, totals)


def swapped(block, axis):
    devices = range(lax.axis_size(axis))
    return lax.ppermute(block, axis, [(i, i ^ 1) for i in devices])


def local(queries, new_kv, own_kv, prompt_kv, out_weight, parents, own_len, first_beam):
    per_dev = queries.shape[0]
    head_dim = HD
    kv_heads_local = new_kv.shape[2] // head_dim
    q_heads_local = queries.shape[1] // head_dim
    group_size = q_heads_local // kv_heads_local
    own_size = own_kv.shape[1]
    prompt_size = prompt_kv.shape[1]
    req_count = lax.axis_size("req")
    beam_count = per_dev * req_count
    dev_index = lax.axis_index("req")
    mate_index = dev_index ^ 1
    chip = dev_index // 2
    shape4 = (per_dev, kv_heads_local, group_size, head_dim)
    cache_rows = per_dev * own_size

    local_rows = jnp.concatenate(
        [own_kv.reshape(cache_rows, 2, -1), prompt_kv[0]], axis=0
    )
    local_kv = jnp.moveaxis(local_rows, 1, 0)
    mate_kv = swapped(local_kv, "req")

    from_prev = shifted(queries, "req", -2)
    from_next = shifted(queries, "req", 2)
    hood_queries = jnp.concatenate([from_prev, queries, from_next], axis=0)
    hood_queries = hood_queries.reshape((3 * per_dev,) + shape4[1:])
    query_block = queries.reshape(shape4)
    hood_count = 3 * per_dev
    slot_ids = jnp.arange(per_dev, dtype=jnp.int32)
    hood_beams = jnp.concatenate(
        [(dev_index + k) * per_dev + slot_ids for k in (-2, 0, 2)]
    )
    in_range = (hood_beams >= 0) & (hood_beams < beam_count)
    pad = 2 * per_dev
    index_rows = jnp.pad(jnp.stack([parents, first_beam, own_len]), ((0, 0), (pad, pad)))
    window = lax.dynamic_slice_in_dim(index_rows, dev_index * per_dev, 5 * per_dev, axis=1)
    hood_index = jnp.concatenate(
        [window[:, 0:per_dev], window[:, 2 * per_dev : 3 * per_dev], window[:, 4 * per_dev :]],
        axis=1,
    )
    parent = hood_index[0]
    home = hood_index[1] // per_dev
    local_len = window[2, pad : pad + per_dev]
    mate_len = lax.dynamic_slice_in_dim(
        window[2], 3 * per_dev - 2 * per_dev * (dev_index % 2), per_dev
    )
    parent_dev = parent // per_dev
    columns = jnp.arange(cache_rows, dtype=jnp.int32)
    column_slot = columns // own_size

    def own_allowed(holder, lengths):
        return (
            (in_range & (parent_dev == holder))[:, None]
            & (column_slot[None, :] == (parent % per_dev)[:, None])
            & (columns % own_size < jnp.repeat(lengths, own_size))[None, :]
        )

    def kv_rows(kv, lo, count):
        keys = kv[0, lo : lo + count].reshape(count, kv_heads_local, head_dim)
        values = kv[1, lo : lo + count].reshape(count, kv_heads_local, head_dim)
        return keys, values

    start = per_dev
    prompt_queries = hood_queries[start:]

    def prompt_allowed(holder):
        here = in_range[start:] & (home[start:] == holder)
        return jnp.broadcast_to(here[:, None], (hood_count - start, prompt_size))

    parts_here = []
    for kv, holder, lengths in ((local_kv, dev_index, local_len), (mate_kv, mate_index, mate_len)):
        keys, values = kv_rows(kv, 0, cache_rows)
        own_part = partial_block(hood_queries, keys, values, own_allowed(holder, lengths))
        keys, values = kv_rows(kv, cache_rows, prompt_size)
        prompt_part = partial_block(prompt_queries, keys, values, prompt_allowed(holder))
        prompt_full = tuple(
            jnp.concatenate([jnp.zeros_like(x[:start]), x], axis=0) for x in prompt_part
        )
        parts_here += [own_part, prompt_full]
    hood_part = merge_all(parts_here)

    fresh_keys = new_kv[:, 0].reshape(per_dev, 1, kv_heads_local, head_dim)
    fresh_values = new_kv[:, 1].reshape(per_dev, 1, kv_heads_local, head_dim)
    fresh_scores = jnp.einsum(
        "nkgd,nskd->nkgs", query_block, fresh_keys, preferred_element_type=jnp.float32
    ) * (head_dim ** (-0.5))
    fresh_part = (
        fresh_values[:, 0, :, None, :].astype(jnp.float32) * jnp.ones_like(fresh_scores),
        fresh_scores[..., 0],
        jnp.ones_like(fresh_scores[..., 0]),
    )

    def rows(part, lo):
        return tuple(x[lo : lo + per_dev] for x in part)

    back_from_next = unpack(shifted(pack(rows(hood_part, 0)), "req", 2), shape4)
    back_from_prev = unpack(shifted(pack(rows(hood_part, 2 * per_dev)), "req", -2), shape4)
    weighted, _, totals = merge_all(
        [fresh_part, rows(hood_part, per_dev), back_from_next, back_from_prev]
    )
    attended = (
        (weighted / totals[..., None])
        .reshape(per_dev, q_heads_local * head_dim)
        .astype(jnp.bfloat16)
    )
    partial_term = jnp.dot(attended, out_weight, preferred_element_type=jnp.float32)

    tp_count = lax.axis_size("tp")
    tp_index = lax.axis_index("tp")
    width = partial_term.shape[1] // tp_count
    chunks = partial_term.reshape(per_dev, tp_count, width).transpose(1, 0, 2)
    got = lax.all_to_all(chunks.astype(jnp.bfloat16), "tp", 0, 0, tiled=True)
    others = jnp.arange(tp_count, dtype=jnp.int32)[:, None, None] != tp_index
    mine = lax.dynamic_slice_in_dim(partial_term, tp_index * width, width, axis=1)
    total = mine + jnp.sum(jnp.where(others, got.astype(jnp.float32), 0.0), axis=0)
    return total.astype(jnp.bfloat16)


def solution(mesh):
    in_specs = (
        P("req", "tp"),
        P("req", None, "tp"),
        P("req", None, None, "tp"),
        P("req", None, None, "tp"),
        P("tp", None),
        P(),
        P(),
        P(),
    )
    out_specs = P("req", "tp")
    return jax.shard_map(local, mesh=mesh, in_specs=in_specs, out_specs=out_specs, check_vma=False)
```

```python
import jax
import jax.numpy as jnp
from jax import lax
from jax.sharding import PartitionSpec as P

HD = 128
MOST_BEAMS = 16


MASKED_SCORE = -1e30


def shifted(block, axis, distance):
    devices = range(lax.axis_size(axis))
    route = [(i + distance, i) for i in devices if i + distance in devices]
    return lax.ppermute(block, axis, route)


def split_weights(weights):
    high = weights.astype(jnp.bfloat16)
    low = (weights - high.astype(jnp.float32)).astype(jnp.bfloat16)
    return high, low


def partial_block(query_block, key_block, value_block, allowed):
    score_scale = query_block.shape[-1] ** (-0.5)
    scores = jnp.einsum(
        "nkgd,skd->nkgs", query_block, key_block, preferred_element_type=jnp.float32
    )
    scores = scores * score_scale
    masked = allowed[:, None, None, :]
    scores = jnp.where(masked, scores, MASKED_SCORE)
    peaks = jnp.max(scores, axis=-1)
    weights = jnp.where(masked, jnp.exp(scores - peaks[..., None]), 0.0)
    totals = jnp.sum(weights, axis=-1)
    high, low = split_weights(weights)
    formula = "nkgs,skd->nkgd"
    weighted = jnp.einsum(
        formula, high, value_block, preferred_element_type=jnp.float32
    ) + jnp.einsum(formula, low, value_block, preferred_element_type=jnp.float32)
    return (weighted, peaks, totals)


def merge_all(parts):
    peaks = [jnp.where(p[2] > 0, p[1], MASKED_SCORE) for p in parts]
    top = peaks[0]
    for pk in peaks[1:]:
        top = jnp.maximum(top, pk)
    weighted = 0.0
    totals = 0.0
    for part, pk in zip(parts, peaks):
        scale = jnp.where(part[2] > 0, jnp.exp(pk - top), 0.0)
        weighted = weighted + part[0] * scale[..., None]
        totals = totals + part[2] * scale
    return (weighted, top, totals)


def pack(part):
    weighted, peaks, totals = part
    n = weighted.shape[0]
    return jnp.concatenate(
        [weighted.reshape(n, -1), peaks.reshape(n, -1), totals.reshape(n, -1)], axis=1
    )


def unpack(packed, shape):
    n, k, g, d = shape
    width = k * g * d
    weighted = packed[:, :width].reshape(n, k, g, d)
    peaks = packed[:, width : width + k * g].reshape(n, k, g)
    totals = packed[:, width + k * g :].reshape(n, k, g)
    return (weighted, peaks, totals)


def swapped(block, axis):
    devices = range(lax.axis_size(axis))
    return lax.ppermute(block, axis, [(i, i ^ 1) for i in devices])


def local(queries, new_kv, own_kv, prompt_kv, out_weight, parents, own_len, first_beam):
    per_dev = queries.shape[0]
    head_dim = HD
    kv_heads_local = new_kv.shape[2] // head_dim
    q_heads_local = queries.shape[1] // head_dim
    group_size = q_heads_local // kv_heads_local
    own_size = own_kv.shape[1]
    prompt_size = prompt_kv.shape[1]
    req_count = lax.axis_size("req")
    beam_count = per_dev * req_count
    dev_index = lax.axis_index("req")
    mate_index = dev_index ^ 1
    chip = dev_index // 2
    shape4 = (per_dev, kv_heads_local, group_size, head_dim)
    cache_rows = per_dev * own_size

    local_rows = jnp.concatenate(
        [own_kv.reshape(cache_rows, 2, -1), prompt_kv[0], new_kv], axis=0
    )
    local_kv = jnp.moveaxis(local_rows, 1, 0)
    mate_kv = swapped(local_kv, "req")

    from_prev = shifted(queries, "req", -2)
    from_next = shifted(queries, "req", 2)
    hood_queries = jnp.concatenate([from_prev, queries, from_next], axis=0)
    hood_queries = hood_queries.reshape((3 * per_dev,) + shape4[1:])
    hood_count = 3 * per_dev
    slot_ids = jnp.arange(per_dev, dtype=jnp.int32)
    hood_beams = jnp.concatenate(
        [(dev_index + k) * per_dev + slot_ids for k in (-2, 0, 2)]
    )
    in_range = (hood_beams >= 0) & (hood_beams < beam_count)
    pad = 2 * per_dev
    index_rows = jnp.pad(jnp.stack([parents, first_beam, own_len]), ((0, 0), (pad, pad)))
    window = lax.dynamic_slice_in_dim(index_rows, dev_index * per_dev, 5 * per_dev, axis=1)
    hood_index = jnp.concatenate(
        [window[:, 0:per_dev], window[:, 2 * per_dev : 3 * per_dev], window[:, 4 * per_dev :]],
        axis=1,
    )
    parent = hood_index[0]
    home = hood_index[1] // per_dev
    local_len = window[2, pad : pad + per_dev]
    mate_len = lax.dynamic_slice_in_dim(
        window[2], 3 * per_dev - 2 * per_dev * (dev_index % 2), per_dev
    )
    parent_dev = parent // per_dev
    columns = jnp.arange(cache_rows, dtype=jnp.int32)
    column_slot = columns // own_size

    kv_count = cache_rows + prompt_size + per_dev
    all_columns = jnp.arange(kv_count, dtype=jnp.int32)
    is_cache = all_columns < cache_rows
    is_prompt = (all_columns >= cache_rows) & (all_columns < cache_rows + prompt_size)
    is_fresh = all_columns >= cache_rows + prompt_size
    column_slot = jnp.where(is_cache, all_columns // own_size, all_columns - cache_rows - prompt_size)
    column_pos = all_columns % own_size
    hood_slot = hood_beams % per_dev

    def allowed_for(holder, lengths):
        column_len = jnp.repeat(lengths, own_size, total_repeat_length=cache_rows)
        column_len = jnp.pad(column_len, (0, kv_count - cache_rows))
        own_ok = (
            (in_range & (parent_dev == holder))[:, None]
            & is_cache[None, :]
            & (column_slot[None, :] == (parent % per_dev)[:, None])
            & (column_pos < column_len)[None, :]
        )
        prompt_ok = (in_range & (home == holder))[:, None] & is_prompt[None, :]
        fresh_ok = (
            (in_range & (hood_beams // per_dev == holder))[:, None]
            & is_fresh[None, :]
            & (column_slot[None, :] == hood_slot[:, None])
        )
        return own_ok | prompt_ok | fresh_ok

    parts_here = []
    for kv, holder, lengths in ((local_kv, dev_index, local_len), (mate_kv, mate_index, mate_len)):
        keys = kv[0].reshape(kv_count, kv_heads_local, head_dim)
        values = kv[1].reshape(kv_count, kv_heads_local, head_dim)
        parts_here.append(partial_block(hood_queries, keys, values, allowed_for(holder, lengths)))
    hood_part = merge_all(parts_here)

    def rows(part, lo):
        return tuple(x[lo : lo + per_dev] for x in part)

    back_from_next = unpack(shifted(pack(rows(hood_part, 0)), "req", 2), shape4)
    back_from_prev = unpack(shifted(pack(rows(hood_part, 2 * per_dev)), "req", -2), shape4)
    weighted, _, totals = merge_all(
        [rows(hood_part, per_dev), back_from_next, back_from_prev]
    )
    attended = (
        (weighted / totals[..., None])
        .reshape(per_dev, q_heads_local * head_dim)
        .astype(jnp.bfloat16)
    )
    partial_term = jnp.dot(attended, out_weight, preferred_element_type=jnp.float32)

    tp_count = lax.axis_size("tp")
    tp_index = lax.axis_index("tp")
    width = partial_term.shape[1] // tp_count
    chunks = partial_term.reshape(per_dev, tp_count, width).transpose(1, 0, 2)
    got = lax.all_to_all(chunks.astype(jnp.bfloat16), "tp", 0, 0, tiled=True)
    others = jnp.arange(tp_count, dtype=jnp.int32)[:, None, None] != tp_index
    mine = lax.dynamic_slice_in_dim(partial_term, tp_index * width, width, axis=1)
    total = mine + jnp.sum(jnp.where(others, got.astype(jnp.float32), 0.0), axis=0)
    return total.astype(jnp.bfloat16)


def solution(mesh):
    in_specs = (
        P("req", "tp"),
        P("req", None, "tp"),
        P("req", None, None, "tp"),
        P("req", None, None, "tp"),
        P("tp", None),
        P(),
        P(),
        P(),
    )
    out_specs = P("req", "tp")
    return jax.shard_map(local, mesh=mesh, in_specs=in_specs, out_specs=out_specs, check_vma=False)
```

```python
import jax
import jax.numpy as jnp
from jax import lax
from jax.sharding import PartitionSpec as P

HD = 128
MOST_BEAMS = 16


MASKED_SCORE = -1e30


def shifted(block, axis, distance):
    devices = range(lax.axis_size(axis))
    route = [(i + distance, i) for i in devices if i + distance in devices]
    return lax.ppermute(block, axis, route)


def split_weights(weights):
    high = weights.astype(jnp.bfloat16)
    low = (weights - high.astype(jnp.float32)).astype(jnp.bfloat16)
    return high, low


def partial_block(query_block, key_block, value_block, allowed):
    score_scale = query_block.shape[-1] ** (-0.5)
    scores = jnp.einsum(
        "nkgd,skd->nkgs", query_block, key_block, preferred_element_type=jnp.float32
    )
    scores = scores * score_scale
    masked = allowed[:, None, None, :]
    scores = jnp.where(masked, scores, MASKED_SCORE)
    peaks = jnp.max(scores, axis=-1)
    weights = jnp.where(masked, jnp.exp(scores - peaks[..., None]), 0.0)
    totals = jnp.sum(weights, axis=-1)
    high, low = split_weights(weights)
    formula = "nkgs,skd->nkgd"
    weighted = jnp.einsum(
        formula, high, value_block, preferred_element_type=jnp.float32
    ) + jnp.einsum(formula, low, value_block, preferred_element_type=jnp.float32)
    return (weighted, peaks, totals)


def merge_all(parts):
    peaks = [jnp.where(p[2] > 0, p[1], MASKED_SCORE) for p in parts]
    top = peaks[0]
    for pk in peaks[1:]:
        top = jnp.maximum(top, pk)
    weighted = 0.0
    totals = 0.0
    for part, pk in zip(parts, peaks):
        scale = jnp.where(part[2] > 0, jnp.exp(pk - top), 0.0)
        weighted = weighted + part[0] * scale[..., None]
        totals = totals + part[2] * scale
    return (weighted, top, totals)


def pack(part):
    weighted, peaks, totals = part
    n = weighted.shape[0]
    return jnp.concatenate(
        [weighted.reshape(n, -1), peaks.reshape(n, -1), totals.reshape(n, -1)], axis=1
    )


def unpack(packed, shape):
    n, k, g, d = shape
    width = k * g * d
    weighted = packed[:, :width].reshape(n, k, g, d)
    peaks = packed[:, width : width + k * g].reshape(n, k, g)
    totals = packed[:, width + k * g :].reshape(n, k, g)
    return (weighted, peaks, totals)


def swapped(block, axis):
    devices = range(lax.axis_size(axis))
    return lax.ppermute(block, axis, [(i, i ^ 1) for i in devices])


def local(queries, new_kv, own_kv, prompt_kv, out_weight, parents, own_len, first_beam):
    per_dev = queries.shape[0]
    head_dim = HD
    kv_heads_local = new_kv.shape[2] // head_dim
    q_heads_local = queries.shape[1] // head_dim
    group_size = q_heads_local // kv_heads_local
    own_size = own_kv.shape[1]
    prompt_size = prompt_kv.shape[1]
    req_count = lax.axis_size("req")
    beam_count = per_dev * req_count
    dev_index = lax.axis_index("req")
    mate_index = dev_index ^ 1
    chip = dev_index // 2
    shape4 = (per_dev, kv_heads_local, group_size, head_dim)
    cache_rows = per_dev * own_size

    local_rows = jnp.concatenate(
        [own_kv.reshape(cache_rows, 2, -1), prompt_kv[0]], axis=0
    )
    local_kv = jnp.moveaxis(local_rows, 1, 0)
    mate_kv = swapped(local_kv, "req")

    from_prev = shifted(queries, "req", -2)
    from_next = shifted(queries, "req", 2)
    hood_queries = jnp.concatenate([from_prev, queries, from_next], axis=0)
    hood_queries = hood_queries.reshape((3 * per_dev,) + shape4[1:])
    query_block = queries.reshape(shape4)
    hood_count = 3 * per_dev
    slot_ids = jnp.arange(per_dev, dtype=jnp.int32)
    hood_beams = jnp.concatenate(
        [(dev_index + k) * per_dev + slot_ids for k in (-2, 0, 2)]
    )
    in_range = (hood_beams >= 0) & (hood_beams < beam_count)
    pad = 2 * per_dev
    index_rows = jnp.pad(jnp.stack([parents, first_beam, own_len]), ((0, 0), (pad, pad)))
    window = lax.dynamic_slice_in_dim(index_rows, dev_index * per_dev, 5 * per_dev, axis=1)
    hood_index = jnp.concatenate(
        [window[:, 0:per_dev], window[:, 2 * per_dev : 3 * per_dev], window[:, 4 * per_dev :]],
        axis=1,
    )
    parent = hood_index[0]
    home = hood_index[1] // per_dev
    local_len = window[2, pad : pad + per_dev]
    mate_len = lax.dynamic_slice_in_dim(
        window[2], 3 * per_dev - 2 * per_dev * (dev_index % 2), per_dev
    )
    parent_dev = parent // per_dev
    columns = jnp.arange(cache_rows, dtype=jnp.int32)
    column_slot = columns // own_size

    kv_count = cache_rows + prompt_size
    all_columns = jnp.arange(kv_count, dtype=jnp.int32)
    is_cache = all_columns < cache_rows
    column_slot = all_columns // own_size
    column_pos = all_columns % own_size

    def allowed_for(holder, lengths):
        column_len = jnp.pad(
            jnp.repeat(lengths, own_size, total_repeat_length=cache_rows), (0, prompt_size)
        )
        own_ok = (
            (in_range & (parent_dev == holder))[:, None]
            & is_cache[None, :]
            & (column_slot[None, :] == (parent % per_dev)[:, None])
            & (column_pos < column_len)[None, :]
        )
        prompt_ok = (in_range & (home == holder))[:, None] & ~is_cache[None, :]
        return own_ok | prompt_ok

    parts_here = []
    for kv, holder, lengths in ((local_kv, dev_index, local_len), (mate_kv, mate_index, mate_len)):
        keys = kv[0].reshape(kv_count, kv_heads_local, head_dim)
        values = kv[1].reshape(kv_count, kv_heads_local, head_dim)
        parts_here.append(partial_block(hood_queries, keys, values, allowed_for(holder, lengths)))
    hood_part = merge_all(parts_here)

    fresh_keys = new_kv[:, 0].reshape(per_dev, 1, kv_heads_local, head_dim)
    fresh_values = new_kv[:, 1].reshape(per_dev, 1, kv_heads_local, head_dim)
    fresh_scores = jnp.einsum(
        "nkgd,nskd->nkgs", query_block, fresh_keys, preferred_element_type=jnp.float32
    ) * (head_dim ** (-0.5))
    fresh_part = (
        fresh_values[:, 0, :, None, :].astype(jnp.float32) * jnp.ones_like(fresh_scores),
        fresh_scores[..., 0],
        jnp.ones_like(fresh_scores[..., 0]),
    )

    def rows(part, lo):
        return tuple(x[lo : lo + per_dev] for x in part)

    back_from_next = unpack(shifted(pack(rows(hood_part, 0)), "req", 2), shape4)
    back_from_prev = unpack(shifted(pack(rows(hood_part, 2 * per_dev)), "req", -2), shape4)
    weighted, _, totals = merge_all(
        [fresh_part, rows(hood_part, per_dev), back_from_next, back_from_prev]
    )
    attended = (
        (weighted / totals[..., None])
        .reshape(per_dev, q_heads_local * head_dim)
        .astype(jnp.bfloat16)
    )
    partial_term = jnp.dot(attended, out_weight, preferred_element_type=jnp.float32)

    tp_count = lax.axis_size("tp")
    tp_index = lax.axis_index("tp")
    width = partial_term.shape[1] // tp_count
    chunks = partial_term.reshape(per_dev, tp_count, width).transpose(1, 0, 2)
    got = lax.all_to_all(chunks.astype(jnp.bfloat16), "tp", 0, 0, tiled=True)
    others = jnp.arange(tp_count, dtype=jnp.int32)[:, None, None] != tp_index
    mine = lax.dynamic_slice_in_dim(partial_term, tp_index * width, width, axis=1)
    total = mine + jnp.sum(jnp.where(others, got.astype(jnp.float32), 0.0), axis=0)
    return total.astype(jnp.bfloat16)


def solution(mesh):
    in_specs = (
        P("req", "tp"),
        P("req", None, "tp"),
        P("req", None, None, "tp"),
        P("req", None, None, "tp"),
        P("tp", None),
        P(),
        P(),
        P(),
    )
    out_specs = P("req", "tp")
    return jax.shard_map(local, mesh=mesh, in_specs=in_specs, out_specs=out_specs, check_vma=False)
```

```python
import jax
import jax.numpy as jnp
from jax import lax
from jax.sharding import PartitionSpec as P

HD = 128
MOST_BEAMS = 16


MASKED_SCORE = -1e30


def shifted(block, axis, distance):
    devices = range(lax.axis_size(axis))
    route = [(i + distance, i) for i in devices if i + distance in devices]
    return lax.ppermute(block, axis, route)


def split_weights(weights):
    high = weights.astype(jnp.bfloat16)
    low = (weights - high.astype(jnp.float32)).astype(jnp.bfloat16)
    return high, low


def partial_block(query_block, key_block, value_block, allowed):
    score_scale = query_block.shape[-1] ** (-0.5)
    scores = jnp.einsum(
        "nkgd,skd->nkgs", query_block, key_block, preferred_element_type=jnp.float32
    )
    scores = scores * score_scale
    masked = allowed[:, None, None, :]
    scores = jnp.where(masked, scores, MASKED_SCORE)
    peaks = jnp.max(scores, axis=-1)
    weights = jnp.where(masked, jnp.exp(scores - peaks[..., None]), 0.0)
    totals = jnp.sum(weights, axis=-1)
    high, low = split_weights(weights)
    formula = "nkgs,skd->nkgd"
    weighted = jnp.einsum(
        formula, high, value_block, preferred_element_type=jnp.float32
    ) + jnp.einsum(formula, low, value_block, preferred_element_type=jnp.float32)
    return (weighted, peaks, totals)


def merge_all(parts):
    peaks = [jnp.where(p[2] > 0, p[1], MASKED_SCORE) for p in parts]
    top = peaks[0]
    for pk in peaks[1:]:
        top = jnp.maximum(top, pk)
    weighted = 0.0
    totals = 0.0
    for part, pk in zip(parts, peaks):
        scale = jnp.where(part[2] > 0, jnp.exp(pk - top), 0.0)
        weighted = weighted + part[0] * scale[..., None]
        totals = totals + part[2] * scale
    return (weighted, top, totals)


def pack(part):
    weighted, peaks, totals = part
    n = weighted.shape[0]
    return jnp.concatenate(
        [weighted.reshape(n, -1), peaks.reshape(n, -1), totals.reshape(n, -1)], axis=1
    )


def unpack(packed, shape):
    n, k, g, d = shape
    width = k * g * d
    weighted = packed[:, :width].reshape(n, k, g, d)
    peaks = packed[:, width : width + k * g].reshape(n, k, g)
    totals = packed[:, width + k * g :].reshape(n, k, g)
    return (weighted, peaks, totals)


def swapped(block, axis):
    devices = range(lax.axis_size(axis))
    return lax.ppermute(block, axis, [(i, i ^ 1) for i in devices])


def local(queries, new_kv, own_kv, prompt_kv, out_weight, parents, own_len, first_beam):
    per_dev = queries.shape[0]
    head_dim = HD
    kv_heads_local = new_kv.shape[2] // head_dim
    q_heads_local = queries.shape[1] // head_dim
    group_size = q_heads_local // kv_heads_local
    own_size = own_kv.shape[1]
    prompt_size = prompt_kv.shape[1]
    req_count = lax.axis_size("req")
    beam_count = per_dev * req_count
    dev_index = lax.axis_index("req")
    mate_index = dev_index ^ 1
    chip = dev_index // 2
    shape4 = (per_dev, kv_heads_local, group_size, head_dim)
    cache_rows = per_dev * own_size

    local_rows = jnp.concatenate(
        [own_kv.reshape(cache_rows, 2, -1), prompt_kv[0]], axis=0
    )
    local_kv = jnp.moveaxis(local_rows, 1, 0)
    mate_kv = swapped(local_kv, "req")

    from_prev = shifted(queries, "req", -2)
    from_next = shifted(queries, "req", 2)
    hood_queries = jnp.concatenate([from_prev, queries, from_next], axis=0)
    hood_queries = hood_queries.reshape((3 * per_dev,) + shape4[1:])
    query_block = queries.reshape(shape4)
    hood_count = 3 * per_dev
    slot_ids = jnp.arange(per_dev, dtype=jnp.int32)
    hood_beams = jnp.concatenate(
        [(dev_index + k) * per_dev + slot_ids for k in (-2, 0, 2)]
    )
    in_range = (hood_beams >= 0) & (hood_beams < beam_count)
    pad = 2 * per_dev
    index_rows = jnp.pad(jnp.stack([parents, first_beam, own_len]), ((0, 0), (pad, pad)))
    window = lax.dynamic_slice_in_dim(index_rows, dev_index * per_dev, 5 * per_dev, axis=1)
    hood_index = jnp.concatenate(
        [window[:, 0:per_dev], window[:, 2 * per_dev : 3 * per_dev], window[:, 4 * per_dev :]],
        axis=1,
    )
    parent = hood_index[0]
    home = hood_index[1] // per_dev
    local_len = window[2, pad : pad + per_dev]
    mate_len = lax.dynamic_slice_in_dim(
        window[2], 3 * per_dev - 2 * per_dev * (dev_index % 2), per_dev
    )
    parent_dev = parent // per_dev
    columns = jnp.arange(cache_rows, dtype=jnp.int32)
    column_slot = columns // own_size

    kv_count = cache_rows + prompt_size
    all_columns = jnp.arange(kv_count, dtype=jnp.int32)
    is_cache = all_columns < cache_rows
    column_slot = all_columns // own_size
    column_pos = all_columns % own_size

    def allowed_for(holder, lengths):
        per_column = jnp.broadcast_to(lengths[:, None], (per_dev, own_size)).reshape(-1)
        column_len = jnp.pad(per_column, (0, prompt_size))
        own_ok = (
            (in_range & (parent_dev == holder))[:, None]
            & is_cache[None, :]
            & (column_slot[None, :] == (parent % per_dev)[:, None])
            & (column_pos < column_len)[None, :]
        )
        prompt_ok = (in_range & (home == holder))[:, None] & ~is_cache[None, :]
        return own_ok | prompt_ok

    parts_here = []
    for kv, holder, lengths in ((local_kv, dev_index, local_len), (mate_kv, mate_index, mate_len)):
        keys = kv[0].reshape(kv_count, kv_heads_local, head_dim)
        values = kv[1].reshape(kv_count, kv_heads_local, head_dim)
        parts_here.append(partial_block(hood_queries, keys, values, allowed_for(holder, lengths)))
    hood_part = merge_all(parts_here)

    fresh_keys = new_kv[:, 0].reshape(per_dev, 1, kv_heads_local, head_dim)
    fresh_values = new_kv[:, 1].reshape(per_dev, 1, kv_heads_local, head_dim)
    fresh_scores = jnp.einsum(
        "nkgd,nskd->nkgs", query_block, fresh_keys, preferred_element_type=jnp.float32
    ) * (head_dim ** (-0.5))
    fresh_part = (
        fresh_values[:, 0, :, None, :].astype(jnp.float32) * jnp.ones_like(fresh_scores),
        fresh_scores[..., 0],
        jnp.ones_like(fresh_scores[..., 0]),
    )

    def rows(part, lo):
        return tuple(x[lo : lo + per_dev] for x in part)

    back_from_next = unpack(shifted(pack(rows(hood_part, 0)), "req", 2), shape4)
    back_from_prev = unpack(shifted(pack(rows(hood_part, 2 * per_dev)), "req", -2), shape4)
    weighted, _, totals = merge_all(
        [fresh_part, rows(hood_part, per_dev), back_from_next, back_from_prev]
    )
    attended = (
        (weighted / totals[..., None])
        .reshape(per_dev, q_heads_local * head_dim)
        .astype(jnp.bfloat16)
    )
    partial_term = jnp.dot(attended, out_weight, preferred_element_type=jnp.float32)

    tp_count = lax.axis_size("tp")
    tp_index = lax.axis_index("tp")
    width = partial_term.shape[1] // tp_count
    chunks = partial_term.reshape(per_dev, tp_count, width).transpose(1, 0, 2)
    got = lax.all_to_all(chunks.astype(jnp.bfloat16), "tp", 0, 0, tiled=True)
    others = jnp.arange(tp_count, dtype=jnp.int32)[:, None, None] != tp_index
    mine = lax.dynamic_slice_in_dim(partial_term, tp_index * width, width, axis=1)
    total = mine + jnp.sum(jnp.where(others, got.astype(jnp.float32), 0.0), axis=0)
    return total.astype(jnp.bfloat16)


def solution(mesh):
    in_specs = (
        P("req", "tp"),
        P("req", None, "tp"),
        P("req", None, None, "tp"),
        P("req", None, None, "tp"),
        P("tp", None),
        P(),
        P(),
        P(),
    )
    out_specs = P("req", "tp")
    return jax.shard_map(local, mesh=mesh, in_specs=in_specs, out_specs=out_specs, check_vma=False)
```

```python
import jax
import jax.numpy as jnp
from jax import lax
from jax.sharding import PartitionSpec as P

HD = 128
MOST_BEAMS = 16


MASKED_SCORE = -1e30


def shifted(block, axis, distance):
    devices = range(lax.axis_size(axis))
    route = [(i + distance, i) for i in devices if i + distance in devices]
    return lax.ppermute(block, axis, route)


def partial_block(query_block, key_block, value_block, allowed):
    score_scale = query_block.shape[-1] ** (-0.5)
    scores = jnp.einsum(
        "nkgd,skd->nkgs", query_block, key_block, preferred_element_type=jnp.float32
    )
    scores = scores * score_scale
    masked = allowed[:, None, None, :]
    scores = jnp.where(masked, scores, MASKED_SCORE)
    peaks = jnp.max(scores, axis=-1)
    weights = jnp.where(masked, jnp.exp(scores - peaks[..., None]), 0.0)
    totals = jnp.sum(weights, axis=-1)
    weighted = jnp.einsum(
        "nkgs,skd->nkgd", weights.astype(jnp.bfloat16), value_block,
        preferred_element_type=jnp.float32,
    )
    return (weighted, peaks, totals)


def merge_all(parts):
    peaks = [jnp.where(p[2] > 0, p[1], MASKED_SCORE) for p in parts]
    top = peaks[0]
    for pk in peaks[1:]:
        top = jnp.maximum(top, pk)
    weighted = 0.0
    totals = 0.0
    for part, pk in zip(parts, peaks):
        scale = jnp.where(part[2] > 0, jnp.exp(pk - top), 0.0)
        weighted = weighted + part[0] * scale[..., None]
        totals = totals + part[2] * scale
    return (weighted, top, totals)


def pack(part):
    weighted, peaks, totals = part
    n = weighted.shape[0]
    return jnp.concatenate(
        [weighted.reshape(n, -1), peaks.reshape(n, -1), totals.reshape(n, -1)], axis=1
    )


def unpack(packed, shape):
    n, k, g, d = shape
    width = k * g * d
    weighted = packed[:, :width].reshape(n, k, g, d)
    peaks = packed[:, width : width + k * g].reshape(n, k, g)
    totals = packed[:, width + k * g :].reshape(n, k, g)
    return (weighted, peaks, totals)


def swapped(block, axis):
    devices = range(lax.axis_size(axis))
    return lax.ppermute(block, axis, [(i, i ^ 1) for i in devices])


def local(queries, new_kv, own_kv, prompt_kv, out_weight, parents, own_len, first_beam):
    per_dev = queries.shape[0]
    head_dim = HD
    kv_heads_local = new_kv.shape[2] // head_dim
    q_heads_local = queries.shape[1] // head_dim
    group_size = q_heads_local // kv_heads_local
    own_size = own_kv.shape[1]
    prompt_size = prompt_kv.shape[1]
    req_count = lax.axis_size("req")
    beam_count = per_dev * req_count
    dev_index = lax.axis_index("req")
    mate_index = dev_index ^ 1
    chip = dev_index // 2
    shape4 = (per_dev, kv_heads_local, group_size, head_dim)
    cache_rows = per_dev * own_size

    local_rows = jnp.concatenate(
        [own_kv.reshape(cache_rows, 2, -1), prompt_kv[0]], axis=0
    )
    local_kv = jnp.moveaxis(local_rows, 1, 0)
    mate_kv = swapped(local_kv, "req")

    from_prev = shifted(queries, "req", -2)
    from_next = shifted(queries, "req", 2)
    hood_queries = jnp.concatenate([from_prev, queries, from_next], axis=0)
    hood_queries = hood_queries.reshape((3 * per_dev,) + shape4[1:])
    query_block = queries.reshape(shape4)
    hood_count = 3 * per_dev
    slot_ids = jnp.arange(per_dev, dtype=jnp.int32)
    hood_beams = jnp.concatenate(
        [(dev_index + k) * per_dev + slot_ids for k in (-2, 0, 2)]
    )
    in_range = (hood_beams >= 0) & (hood_beams < beam_count)
    pad = 2 * per_dev
    index_rows = jnp.pad(jnp.stack([parents, first_beam, own_len]), ((0, 0), (pad, pad)))
    window = lax.dynamic_slice_in_dim(index_rows, dev_index * per_dev, 5 * per_dev, axis=1)
    hood_index = jnp.concatenate(
        [window[:, 0:per_dev], window[:, 2 * per_dev : 3 * per_dev], window[:, 4 * per_dev :]],
        axis=1,
    )
    parent = hood_index[0]
    home = hood_index[1] // per_dev
    local_len = window[2, pad : pad + per_dev]
    mate_len = lax.dynamic_slice_in_dim(
        window[2], 3 * per_dev - 2 * per_dev * (dev_index % 2), per_dev
    )
    parent_dev = parent // per_dev
    columns = jnp.arange(cache_rows, dtype=jnp.int32)
    column_slot = columns // own_size

    kv_count = cache_rows + prompt_size
    all_columns = jnp.arange(kv_count, dtype=jnp.int32)
    is_cache = all_columns < cache_rows
    column_slot = all_columns // own_size
    column_pos = all_columns % own_size

    def allowed_for(holder, lengths):
        per_column = jnp.broadcast_to(lengths[:, None], (per_dev, own_size)).reshape(-1)
        column_len = jnp.pad(per_column, (0, prompt_size))
        own_ok = (
            (in_range & (parent_dev == holder))[:, None]
            & is_cache[None, :]
            & (column_slot[None, :] == (parent % per_dev)[:, None])
            & (column_pos < column_len)[None, :]
        )
        prompt_ok = (in_range & (home == holder))[:, None] & ~is_cache[None, :]
        return own_ok | prompt_ok

    parts_here = []
    for kv, holder, lengths in ((local_kv, dev_index, local_len), (mate_kv, mate_index, mate_len)):
        keys = kv[0].reshape(kv_count, kv_heads_local, head_dim)
        values = kv[1].reshape(kv_count, kv_heads_local, head_dim)
        parts_here.append(partial_block(hood_queries, keys, values, allowed_for(holder, lengths)))
    hood_part = merge_all(parts_here)

    fresh_keys = new_kv[:, 0].reshape(per_dev, 1, kv_heads_local, head_dim)
    fresh_values = new_kv[:, 1].reshape(per_dev, 1, kv_heads_local, head_dim)
    fresh_scores = jnp.einsum(
        "nkgd,nskd->nkgs", query_block, fresh_keys, preferred_element_type=jnp.float32
    ) * (head_dim ** (-0.5))
    fresh_part = (
        fresh_values[:, 0, :, None, :].astype(jnp.float32) * jnp.ones_like(fresh_scores),
        fresh_scores[..., 0],
        jnp.ones_like(fresh_scores[..., 0]),
    )

    def rows(part, lo):
        return tuple(x[lo : lo + per_dev] for x in part)

    back_from_next = unpack(shifted(pack(rows(hood_part, 0)), "req", 2), shape4)
    back_from_prev = unpack(shifted(pack(rows(hood_part, 2 * per_dev)), "req", -2), shape4)
    weighted, _, totals = merge_all(
        [fresh_part, rows(hood_part, per_dev), back_from_next, back_from_prev]
    )
    attended = (
        (weighted / totals[..., None])
        .reshape(per_dev, q_heads_local * head_dim)
        .astype(jnp.bfloat16)
    )
    partial_term = jnp.dot(attended, out_weight, preferred_element_type=jnp.float32)

    tp_count = lax.axis_size("tp")
    tp_index = lax.axis_index("tp")
    width = partial_term.shape[1] // tp_count
    chunks = partial_term.reshape(per_dev, tp_count, width).transpose(1, 0, 2)
    got = lax.all_to_all(chunks.astype(jnp.bfloat16), "tp", 0, 0, tiled=True)
    others = jnp.arange(tp_count, dtype=jnp.int32)[:, None, None] != tp_index
    mine = lax.dynamic_slice_in_dim(partial_term, tp_index * width, width, axis=1)
    total = mine + jnp.sum(jnp.where(others, got.astype(jnp.float32), 0.0), axis=0)
    return total.astype(jnp.bfloat16)


def solution(mesh):
    in_specs = (
        P("req", "tp"),
        P("req", None, "tp"),
        P("req", None, None, "tp"),
        P("req", None, None, "tp"),
        P("tp", None),
        P(),
        P(),
        P(),
    )
    out_specs = P("req", "tp")
    return jax.shard_map(local, mesh=mesh, in_specs=in_specs, out_specs=out_specs, check_vma=False)
```

```python
import jax
import jax.numpy as jnp
from jax import lax
from jax.sharding import PartitionSpec as P

HD = 128
MOST_BEAMS = 16


MASKED_SCORE = -1e30


def shifted(block, axis, distance):
    devices = range(lax.axis_size(axis))
    route = [(i + distance, i) for i in devices if i + distance in devices]
    return lax.ppermute(block, axis, route)


def partial_block(query_block, key_block, value_block, allowed):
    score_scale = query_block.shape[-1] ** (-0.5)
    scores = jnp.einsum(
        "nkgd,skd->nkgs", query_block, key_block, preferred_element_type=jnp.float32
    )
    scores = scores * score_scale
    masked = allowed[:, None, None, :]
    scores = jnp.where(masked, scores, MASKED_SCORE)
    peaks = jnp.max(scores, axis=-1)
    weights = jnp.where(masked, jnp.exp(scores - peaks[..., None]), 0.0)
    totals = jnp.sum(weights, axis=-1)
    weighted = jnp.einsum(
        "nkgs,skd->nkgd", weights.astype(jnp.bfloat16), value_block,
        preferred_element_type=jnp.float32,
    )
    return (weighted, peaks, totals)


def merge_all(parts):
    peaks = [jnp.where(p[2] > 0, p[1], MASKED_SCORE) for p in parts]
    top = peaks[0]
    for pk in peaks[1:]:
        top = jnp.maximum(top, pk)
    weighted = 0.0
    totals = 0.0
    for part, pk in zip(parts, peaks):
        scale = jnp.where(part[2] > 0, jnp.exp(pk - top), 0.0)
        weighted = weighted + part[0] * scale[..., None]
        totals = totals + part[2] * scale
    return (weighted, top, totals)


def pack(part):
    weighted, peaks, totals = part
    n = weighted.shape[0]
    return jnp.concatenate(
        [weighted.reshape(n, -1), peaks.reshape(n, -1), totals.reshape(n, -1)], axis=1
    )


def unpack(packed, shape):
    n, k, g, d = shape
    width = k * g * d
    weighted = packed[:, :width].reshape(n, k, g, d)
    peaks = packed[:, width : width + k * g].reshape(n, k, g)
    totals = packed[:, width + k * g :].reshape(n, k, g)
    return (weighted, peaks, totals)


def swapped(block, axis):
    devices = range(lax.axis_size(axis))
    return lax.ppermute(block, axis, [(i, i ^ 1) for i in devices])


def local(queries, new_kv, own_kv, prompt_kv, out_weight, parents, own_len, first_beam):
    per_dev = queries.shape[0]
    head_dim = HD
    kv_heads_local = new_kv.shape[2] // head_dim
    q_heads_local = queries.shape[1] // head_dim
    group_size = q_heads_local // kv_heads_local
    own_size = own_kv.shape[1]
    prompt_size = prompt_kv.shape[1]
    req_count = lax.axis_size("req")
    beam_count = per_dev * req_count
    dev_index = lax.axis_index("req")
    mate_index = dev_index ^ 1
    chip = dev_index // 2
    shape4 = (per_dev, kv_heads_local, group_size, head_dim)
    cache_rows = per_dev * own_size

    local_rows = jnp.concatenate(
        [own_kv.reshape(cache_rows, 2, -1), prompt_kv[0], new_kv], axis=0
    )
    local_kv = jnp.moveaxis(local_rows, 1, 0)
    mate_kv = swapped(local_kv, "req")

    from_prev = shifted(queries, "req", -2)
    from_next = shifted(queries, "req", 2)
    hood_queries = jnp.concatenate([from_prev, queries, from_next], axis=0)
    hood_queries = hood_queries.reshape((3 * per_dev,) + shape4[1:])
    hood_count = 3 * per_dev
    slot_ids = jnp.arange(per_dev, dtype=jnp.int32)
    hood_beams = jnp.concatenate(
        [(dev_index + k) * per_dev + slot_ids for k in (-2, 0, 2)]
    )
    in_range = (hood_beams >= 0) & (hood_beams < beam_count)
    pad = 2 * per_dev
    index_rows = jnp.pad(jnp.stack([parents, first_beam, own_len]), ((0, 0), (pad, pad)))
    window = lax.dynamic_slice_in_dim(index_rows, dev_index * per_dev, 5 * per_dev, axis=1)
    hood_index = jnp.concatenate(
        [window[:, 0:per_dev], window[:, 2 * per_dev : 3 * per_dev], window[:, 4 * per_dev :]],
        axis=1,
    )
    parent = hood_index[0]
    home = hood_index[1] // per_dev
    local_len = window[2, pad : pad + per_dev]
    mate_len = lax.dynamic_slice_in_dim(
        window[2], 3 * per_dev - 2 * per_dev * (dev_index % 2), per_dev
    )
    parent_dev = parent // per_dev
    columns = jnp.arange(cache_rows, dtype=jnp.int32)
    column_slot = columns // own_size

    kv_count = cache_rows + prompt_size + per_dev
    all_columns = jnp.arange(kv_count, dtype=jnp.int32)
    is_cache = all_columns < cache_rows
    is_prompt = (all_columns >= cache_rows) & (all_columns < cache_rows + prompt_size)
    is_fresh = all_columns >= cache_rows + prompt_size
    column_slot = jnp.where(is_cache, all_columns // own_size, all_columns - cache_rows - prompt_size)
    column_pos = all_columns % own_size
    hood_slot = hood_beams % per_dev

    def allowed_for(holder, lengths):
        per_column = jnp.broadcast_to(lengths[:, None], (per_dev, own_size)).reshape(-1)
        column_len = jnp.pad(per_column, (0, kv_count - cache_rows))
        own_ok = (
            (in_range & (parent_dev == holder))[:, None]
            & is_cache[None, :]
            & (column_slot[None, :] == (parent % per_dev)[:, None])
            & (column_pos < column_len)[None, :]
        )
        prompt_ok = (in_range & (home == holder))[:, None] & is_prompt[None, :]
        fresh_ok = (
            (in_range & (hood_beams // per_dev == holder))[:, None]
            & is_fresh[None, :]
            & (column_slot[None, :] == hood_slot[:, None])
        )
        return own_ok | prompt_ok | fresh_ok

    parts_here = []
    for kv, holder, lengths in ((local_kv, dev_index, local_len), (mate_kv, mate_index, mate_len)):
        keys = kv[0].reshape(kv_count, kv_heads_local, head_dim)
        values = kv[1].reshape(kv_count, kv_heads_local, head_dim)
        parts_here.append(partial_block(hood_queries, keys, values, allowed_for(holder, lengths)))
    hood_part = merge_all(parts_here)

    def rows(part, lo):
        return tuple(x[lo : lo + per_dev] for x in part)

    back_from_next = unpack(shifted(pack(rows(hood_part, 0)), "req", 2), shape4)
    back_from_prev = unpack(shifted(pack(rows(hood_part, 2 * per_dev)), "req", -2), shape4)
    weighted, _, totals = merge_all(
        [rows(hood_part, per_dev), back_from_next, back_from_prev]
    )
    attended = (
        (weighted / totals[..., None])
        .reshape(per_dev, q_heads_local * head_dim)
        .astype(jnp.bfloat16)
    )
    partial_term = jnp.dot(attended, out_weight, preferred_element_type=jnp.float32)

    tp_count = lax.axis_size("tp")
    tp_index = lax.axis_index("tp")
    width = partial_term.shape[1] // tp_count
    chunks = partial_term.reshape(per_dev, tp_count, width).transpose(1, 0, 2)
    got = lax.all_to_all(chunks.astype(jnp.bfloat16), "tp", 0, 0, tiled=True)
    others = jnp.arange(tp_count, dtype=jnp.int32)[:, None, None] != tp_index
    mine = lax.dynamic_slice_in_dim(partial_term, tp_index * width, width, axis=1)
    total = mine + jnp.sum(jnp.where(others, got.astype(jnp.float32), 0.0), axis=0)
    return total.astype(jnp.bfloat16)


def solution(mesh):
    in_specs = (
        P("req", "tp"),
        P("req", None, "tp"),
        P("req", None, None, "tp"),
        P("req", None, None, "tp"),
        P("tp", None),
        P(),
        P(),
        P(),
    )
    out_specs = P("req", "tp")
    return jax.shard_map(local, mesh=mesh, in_specs=in_specs, out_specs=out_specs, check_vma=False)
```

```python
import functools

import jax
import jax.numpy as jnp
from jax import lax
from jax.experimental import pallas as pl
from jax.sharding import PartitionSpec as P

HD = 128
MOST_BEAMS = 16


MASKED_SCORE = -1e30


def shifted(block, axis, distance):
    devices = range(lax.axis_size(axis))
    route = [(i + distance, i) for i in devices if i + distance in devices]
    return lax.ppermute(block, axis, route)


def partial_block(query_block, key_block, value_block, allowed):
    score_scale = query_block.shape[-1] ** (-0.5)
    scores = jnp.einsum(
        "nkgd,skd->nkgs", query_block, key_block, preferred_element_type=jnp.float32
    )
    scores = scores * score_scale
    masked = allowed[:, None, None, :]
    scores = jnp.where(masked, scores, MASKED_SCORE)
    peaks = jnp.max(scores, axis=-1)
    weights = jnp.where(masked, jnp.exp(scores - peaks[..., None]), 0.0)
    totals = jnp.sum(weights, axis=-1)
    weighted = jnp.einsum(
        "nkgs,skd->nkgd", weights.astype(jnp.bfloat16), value_block,
        preferred_element_type=jnp.float32,
    )
    return (weighted, peaks, totals)


def merge_all(parts):
    peaks = [jnp.where(p[2] > 0, p[1], MASKED_SCORE) for p in parts]
    top = peaks[0]
    for pk in peaks[1:]:
        top = jnp.maximum(top, pk)
    weighted = 0.0
    totals = 0.0
    for part, pk in zip(parts, peaks):
        scale = jnp.where(part[2] > 0, jnp.exp(pk - top), 0.0)
        weighted = weighted + part[0] * scale[..., None]
        totals = totals + part[2] * scale
    return (weighted, top, totals)


def pack(part):
    weighted, peaks, totals = part
    n = weighted.shape[0]
    return jnp.concatenate(
        [weighted.reshape(n, -1), peaks.reshape(n, -1), totals.reshape(n, -1)], axis=1
    )


def unpack(packed, shape):
    n, k, g, d = shape
    width = k * g * d
    weighted = packed[:, :width].reshape(n, k, g, d)
    peaks = packed[:, width : width + k * g].reshape(n, k, g)
    totals = packed[:, width + k * g :].reshape(n, k, g)
    return (weighted, peaks, totals)


def attend_kernel(q_ref, local_ref, mate_ref, row_ref, w_ref, peak_ref, total_ref, *, cache_rows, slot_shift):
    queries = q_ref[...]
    rows = row_ref[...]
    shape = (queries.shape[0], local_ref.shape[1])
    columns = lax.broadcasted_iota(jnp.int32, shape, 1)
    is_cache = columns < cache_rows
    column_slot = jnp.right_shift(columns, slot_shift)
    column_pos = jnp.bitwise_and(columns, (1 << slot_shift) - 1)
    score_scale = queries.shape[-1] ** (-0.5)

    def part(kv_ref, base):
        scores = lax.dot_general(
            queries, kv_ref[0], (((1,), (1,)), ((), ())), preferred_element_type=jnp.float32
        ) * score_scale
        slot = rows[:, base : base + 1]
        length = rows[:, base + 1 : base + 2]
        prompt_ok = rows[:, base + 2 : base + 3] > 0
        allowed = (is_cache & (column_slot == slot) & (column_pos < length)) | (
            jnp.logical_not(is_cache) & prompt_ok
        )
        scores = jnp.where(allowed, scores, MASKED_SCORE)
        peak = jnp.max(scores, axis=1, keepdims=True)
        weights = jnp.where(allowed, jnp.exp(scores - peak), 0.0)
        total = jnp.sum(weights, axis=1, keepdims=True)
        weighted = jnp.dot(
            weights.astype(jnp.bfloat16), kv_ref[1], preferred_element_type=jnp.float32
        )
        return weighted, jnp.where(total > 0, peak, MASKED_SCORE), total

    w_local, p_local, t_local = part(local_ref, 0)
    w_mate, p_mate, t_mate = part(mate_ref, 3)
    top = jnp.maximum(p_local, p_mate)
    s_local = jnp.where(t_local > 0, jnp.exp(p_local - top), 0.0)
    s_mate = jnp.where(t_mate > 0, jnp.exp(p_mate - top), 0.0)
    w_ref[...] = w_local * s_local + w_mate * s_mate
    peak_ref[...] = jnp.broadcast_to(top, peak_ref.shape)
    total_ref[...] = jnp.broadcast_to(t_local * s_local + t_mate * s_mate, total_ref.shape)


def attend(queries, local_kv, mate_kv, row_params, cache_rows, own_size):
    count, width = queries.shape
    slot_shift = own_size.bit_length() - 1
    assert 1 << slot_shift == own_size
    body = functools.partial(attend_kernel, cache_rows=cache_rows, slot_shift=slot_shift)
    return pl.pallas_call(
        body,
        out_shape=(
            jax.ShapeDtypeStruct((count, width), jnp.float32),
            jax.ShapeDtypeStruct((count, 128), jnp.float32),
            jax.ShapeDtypeStruct((count, 128), jnp.float32),
        ),
    )(queries, local_kv, mate_kv, row_params)


def swapped(block, axis):
    devices = range(lax.axis_size(axis))
    return lax.ppermute(block, axis, [(i, i ^ 1) for i in devices])


def local(queries, new_kv, own_kv, prompt_kv, out_weight, parents, own_len, first_beam):
    per_dev = queries.shape[0]
    head_dim = HD
    kv_heads_local = new_kv.shape[2] // head_dim
    q_heads_local = queries.shape[1] // head_dim
    group_size = q_heads_local // kv_heads_local
    own_size = own_kv.shape[1]
    prompt_size = prompt_kv.shape[1]
    req_count = lax.axis_size("req")
    beam_count = per_dev * req_count
    dev_index = lax.axis_index("req")
    mate_index = dev_index ^ 1
    chip = dev_index // 2
    shape4 = (per_dev, kv_heads_local, group_size, head_dim)
    cache_rows = per_dev * own_size

    local_rows = jnp.concatenate(
        [own_kv.reshape(cache_rows, 2, -1), prompt_kv[0]], axis=0
    )
    local_kv = jnp.moveaxis(local_rows, 1, 0)
    mate_kv = swapped(local_kv, "req")

    from_prev = shifted(queries, "req", -2)
    from_next = shifted(queries, "req", 2)
    hood_queries = jnp.concatenate([from_prev, queries, from_next], axis=0)
    hood_queries = hood_queries.reshape((3 * per_dev,) + shape4[1:])
    query_block = queries.reshape(shape4)
    hood_count = 3 * per_dev
    slot_ids = jnp.arange(per_dev, dtype=jnp.int32)
    hood_beams = jnp.concatenate(
        [(dev_index + k) * per_dev + slot_ids for k in (-2, 0, 2)]
    )
    in_range = (hood_beams >= 0) & (hood_beams < beam_count)
    pad = 2 * per_dev
    index_rows = jnp.pad(jnp.stack([parents, first_beam, own_len]), ((0, 0), (pad, pad)))
    window = lax.dynamic_slice_in_dim(index_rows, dev_index * per_dev, 5 * per_dev, axis=1)
    hood_index = jnp.concatenate(
        [window[:, 0:per_dev], window[:, 2 * per_dev : 3 * per_dev], window[:, 4 * per_dev :]],
        axis=1,
    )
    parent = hood_index[0]
    home = hood_index[1] // per_dev
    local_len = window[2, pad : pad + per_dev]
    mate_len = lax.dynamic_slice_in_dim(
        window[2], 3 * per_dev - 2 * per_dev * (dev_index % 2), per_dev
    )
    parent_dev = parent // per_dev
    assert kv_heads_local == 1
    slot_onehot = (parent % per_dev)[:, None] == slot_ids[None, :]
    params = []
    for holder, lengths in ((dev_index, local_len), (mate_index, mate_len)):
        held = in_range & (parent_dev == holder)
        params += [
            jnp.where(held, parent % per_dev, -1),
            jnp.sum(jnp.where(slot_onehot, lengths[None, :], 0), axis=1),
            (in_range & (home == holder)).astype(jnp.int32),
        ]
    params += [jnp.zeros_like(parent), jnp.zeros_like(parent)]
    beam_params = jnp.stack(params, axis=1)
    row_params = jnp.broadcast_to(
        beam_params[:, None, :], (hood_count, group_size, beam_params.shape[1])
    ).reshape(hood_count * group_size, -1)
    weighted_rows, peak_rows, total_rows = attend(
        hood_queries.reshape(hood_count * group_size, head_dim),
        local_kv, mate_kv, row_params, cache_rows, own_size,
    )
    hood_part = (
        weighted_rows.reshape(hood_count, kv_heads_local, group_size, head_dim),
        peak_rows[:, 0].reshape(hood_count, kv_heads_local, group_size),
        total_rows[:, 0].reshape(hood_count, kv_heads_local, group_size),
    )

    fresh_keys = new_kv[:, 0].reshape(per_dev, 1, kv_heads_local, head_dim)
    fresh_values = new_kv[:, 1].reshape(per_dev, 1, kv_heads_local, head_dim)
    fresh_scores = jnp.einsum(
        "nkgd,nskd->nkgs", query_block, fresh_keys, preferred_element_type=jnp.float32
    ) * (head_dim ** (-0.5))
    fresh_part = (
        fresh_values[:, 0, :, None, :].astype(jnp.float32) * jnp.ones_like(fresh_scores),
        fresh_scores[..., 0],
        jnp.ones_like(fresh_scores[..., 0]),
    )

    def rows(part, lo):
        return tuple(x[lo : lo + per_dev] for x in part)

    back_from_next = unpack(shifted(pack(rows(hood_part, 0)), "req", 2), shape4)
    back_from_prev = unpack(shifted(pack(rows(hood_part, 2 * per_dev)), "req", -2), shape4)
    weighted, _, totals = merge_all(
        [fresh_part, rows(hood_part, per_dev), back_from_next, back_from_prev]
    )
    attended = (
        (weighted / totals[..., None])
        .reshape(per_dev, q_heads_local * head_dim)
        .astype(jnp.bfloat16)
    )
    partial_term = jnp.dot(attended, out_weight, preferred_element_type=jnp.float32)

    tp_count = lax.axis_size("tp")
    tp_index = lax.axis_index("tp")
    width = partial_term.shape[1] // tp_count
    chunks = partial_term.reshape(per_dev, tp_count, width).transpose(1, 0, 2)
    got = lax.all_to_all(chunks.astype(jnp.bfloat16), "tp", 0, 0, tiled=True)
    others = jnp.arange(tp_count, dtype=jnp.int32)[:, None, None] != tp_index
    mine = lax.dynamic_slice_in_dim(partial_term, tp_index * width, width, axis=1)
    total = mine + jnp.sum(jnp.where(others, got.astype(jnp.float32), 0.0), axis=0)
    return total.astype(jnp.bfloat16)


def solution(mesh):
    in_specs = (
        P("req", "tp"),
        P("req", None, "tp"),
        P("req", None, None, "tp"),
        P("req", None, None, "tp"),
        P("tp", None),
        P(),
        P(),
        P(),
    )
    out_specs = P("req", "tp")
    return jax.shard_map(local, mesh=mesh, in_specs=in_specs, out_specs=out_specs, check_vma=False)
```

```python
import jax
import jax.numpy as jnp
from jax import lax
from jax.sharding import PartitionSpec as P

HD = 128
MOST_BEAMS = 16


MASKED_SCORE = -1e30


def shifted(block, axis, distance):
    devices = range(lax.axis_size(axis))
    route = [(i + distance, i) for i in devices if i + distance in devices]
    return lax.ppermute(block, axis, route)


def partial_block(query_block, key_block, value_block, allowed):
    score_scale = query_block.shape[-1] ** (-0.5)
    scores = jnp.einsum(
        "nkgd,skd->nkgs", query_block, key_block, preferred_element_type=jnp.float32
    )
    scores = scores * score_scale
    masked = allowed[:, None, None, :]
    scores = jnp.where(masked, scores, MASKED_SCORE)
    peaks = jnp.max(scores, axis=-1)
    weights = jnp.where(masked, jnp.exp(scores - peaks[..., None]), 0.0)
    totals = jnp.sum(weights, axis=-1)
    weighted = jnp.einsum(
        "nkgs,skd->nkgd", weights.astype(jnp.bfloat16), value_block,
        preferred_element_type=jnp.float32,
    )
    return (weighted, peaks, totals)


def merge_all(parts):
    peaks = [jnp.where(p[2] > 0, p[1], MASKED_SCORE) for p in parts]
    top = peaks[0]
    for pk in peaks[1:]:
        top = jnp.maximum(top, pk)
    weighted = 0.0
    totals = 0.0
    for part, pk in zip(parts, peaks):
        scale = jnp.where(part[2] > 0, jnp.exp(pk - top), 0.0)
        weighted = weighted + part[0] * scale[..., None]
        totals = totals + part[2] * scale
    return (weighted, top, totals)


def pack(part):
    weighted, peaks, totals = part
    n = weighted.shape[0]
    return jnp.concatenate(
        [weighted.reshape(n, -1), peaks.reshape(n, -1), totals.reshape(n, -1)], axis=1
    )


def unpack(packed, shape):
    n, k, g, d = shape
    width = k * g * d
    weighted = packed[:, :width].reshape(n, k, g, d)
    peaks = packed[:, width : width + k * g].reshape(n, k, g)
    totals = packed[:, width + k * g :].reshape(n, k, g)
    return (weighted, peaks, totals)


def swapped(block, axis):
    devices = range(lax.axis_size(axis))
    return lax.ppermute(block, axis, [(i, i ^ 1) for i in devices])


def local(queries, new_kv, own_kv, prompt_kv, out_weight, parents, own_len, first_beam):
    per_dev = queries.shape[0]
    head_dim = HD
    kv_heads_local = new_kv.shape[2] // head_dim
    q_heads_local = queries.shape[1] // head_dim
    group_size = q_heads_local // kv_heads_local
    own_size = own_kv.shape[1]
    prompt_size = prompt_kv.shape[1]
    req_count = lax.axis_size("req")
    beam_count = per_dev * req_count
    dev_index = lax.axis_index("req")
    mate_index = dev_index ^ 1
    chip = dev_index // 2
    shape4 = (per_dev, kv_heads_local, group_size, head_dim)
    cache_rows = per_dev * own_size

    local_rows = jnp.concatenate(
        [own_kv.reshape(cache_rows, 2, -1), prompt_kv[0]], axis=0
    )
    local_kv = jnp.moveaxis(local_rows, 1, 0)
    mate_kv = swapped(local_kv, "req")

    from_prev = shifted(queries, "req", -2)
    from_next = shifted(queries, "req", 2)
    hood_queries = jnp.concatenate([from_prev, queries, from_next], axis=0)
    hood_queries = hood_queries.reshape((3 * per_dev,) + shape4[1:])
    query_block = queries.reshape(shape4)
    hood_count = 3 * per_dev
    slot_ids = jnp.arange(per_dev, dtype=jnp.int32)
    hood_beams = jnp.concatenate(
        [(dev_index + k) * per_dev + slot_ids for k in (-2, 0, 2)]
    )
    in_range = (hood_beams >= 0) & (hood_beams < beam_count)
    pad = 2 * per_dev
    index_rows = jnp.pad(jnp.stack([parents, first_beam, own_len]), ((0, 0), (pad, pad)))
    window = lax.dynamic_slice_in_dim(index_rows, dev_index * per_dev, 5 * per_dev, axis=1)
    hood_index = jnp.concatenate(
        [window[:, 0:per_dev], window[:, 2 * per_dev : 3 * per_dev], window[:, 4 * per_dev :]],
        axis=1,
    )
    parent = hood_index[0]
    home = hood_index[1] // per_dev
    local_len = window[2, pad : pad + per_dev]
    mate_len = lax.dynamic_slice_in_dim(
        window[2], 3 * per_dev - 2 * per_dev * (dev_index % 2), per_dev
    )
    parent_dev = parent // per_dev
    columns = jnp.arange(cache_rows, dtype=jnp.int32)
    column_slot = columns // own_size

    kv_count = cache_rows + prompt_size
    all_columns = jnp.arange(kv_count, dtype=jnp.int32)
    is_cache = all_columns < cache_rows
    column_slot = all_columns // own_size
    column_pos = all_columns % own_size

    def allowed_for(holder, lengths):
        per_column = jnp.broadcast_to(lengths[:, None], (per_dev, own_size)).reshape(-1)
        column_len = jnp.pad(per_column, (0, prompt_size))
        own_ok = (
            (in_range & (parent_dev == holder))[:, None]
            & is_cache[None, :]
            & (column_slot[None, :] == (parent % per_dev)[:, None])
            & (column_pos < column_len)[None, :]
        )
        prompt_ok = (in_range & (home == holder))[:, None] & ~is_cache[None, :]
        return own_ok | prompt_ok

    def pick_rows(x, groups):
        return jnp.concatenate([x[g * per_dev : (g + 1) * per_dev] for g in groups], axis=0)

    send_parts = []
    own_parts = []
    for kv, holder, lengths in ((local_kv, dev_index, local_len), (mate_kv, mate_index, mate_len)):
        keys = kv[0].reshape(kv_count, kv_heads_local, head_dim)
        values = kv[1].reshape(kv_count, kv_heads_local, head_dim)
        allowed = allowed_for(holder, lengths)
        send_parts.append(
            partial_block(pick_rows(hood_queries, (0, 2)), keys, values, pick_rows(allowed, (0, 2)))
        )
        own_parts.append(
            partial_block(pick_rows(hood_queries, (1,)), keys, values, pick_rows(allowed, (1,)))
        )
    send_part = merge_all(send_parts)

    fresh_keys = new_kv[:, 0].reshape(per_dev, 1, kv_heads_local, head_dim)
    fresh_values = new_kv[:, 1].reshape(per_dev, 1, kv_heads_local, head_dim)
    fresh_scores = jnp.einsum(
        "nkgd,nskd->nkgs", query_block, fresh_keys, preferred_element_type=jnp.float32
    ) * (head_dim ** (-0.5))
    fresh_part = (
        fresh_values[:, 0, :, None, :].astype(jnp.float32) * jnp.ones_like(fresh_scores),
        fresh_scores[..., 0],
        jnp.ones_like(fresh_scores[..., 0]),
    )

    def rows(part, lo):
        return tuple(x[lo : lo + per_dev] for x in part)

    back_from_next = unpack(shifted(pack(rows(send_part, 0)), "req", 2), shape4)
    back_from_prev = unpack(shifted(pack(rows(send_part, per_dev)), "req", -2), shape4)
    weighted, _, totals = merge_all(
        [fresh_part] + own_parts + [back_from_next, back_from_prev]
    )
    attended = (
        (weighted / totals[..., None])
        .reshape(per_dev, q_heads_local * head_dim)
        .astype(jnp.bfloat16)
    )
    partial_term = jnp.dot(attended, out_weight, preferred_element_type=jnp.float32)

    tp_count = lax.axis_size("tp")
    tp_index = lax.axis_index("tp")
    width = partial_term.shape[1] // tp_count
    chunks = partial_term.reshape(per_dev, tp_count, width).transpose(1, 0, 2)
    got = lax.all_to_all(chunks.astype(jnp.bfloat16), "tp", 0, 0, tiled=True)
    others = jnp.arange(tp_count, dtype=jnp.int32)[:, None, None] != tp_index
    mine = lax.dynamic_slice_in_dim(partial_term, tp_index * width, width, axis=1)
    total = mine + jnp.sum(jnp.where(others, got.astype(jnp.float32), 0.0), axis=0)
    return total.astype(jnp.bfloat16)


def solution(mesh):
    in_specs = (
        P("req", "tp"),
        P("req", None, "tp"),
        P("req", None, None, "tp"),
        P("req", None, None, "tp"),
        P("tp", None),
        P(),
        P(),
        P(),
    )
    out_specs = P("req", "tp")
    return jax.shard_map(local, mesh=mesh, in_specs=in_specs, out_specs=out_specs, check_vma=False)
```

```python
import jax
import jax.numpy as jnp
from jax import lax
from jax.sharding import PartitionSpec as P

HD = 128
MOST_BEAMS = 16


MASKED_SCORE = -1e30


def shifted(block, axis, distance):
    devices = range(lax.axis_size(axis))
    route = [(i + distance, i) for i in devices if i + distance in devices]
    return lax.ppermute(block, axis, route)


def partial_block(query_block, key_block, value_block, allowed):
    score_scale = query_block.shape[-1] ** (-0.5)
    scores = jnp.einsum(
        "nkgd,skd->nkgs", query_block, key_block, preferred_element_type=jnp.float32
    )
    scores = scores * score_scale
    masked = allowed[:, None, None, :]
    scores = jnp.where(masked, scores, MASKED_SCORE)
    peaks = jnp.max(scores, axis=-1)
    weights = jnp.where(masked, jnp.exp(scores - peaks[..., None]), 0.0)
    totals = jnp.sum(weights, axis=-1)
    weighted = jnp.einsum(
        "nkgs,skd->nkgd", weights.astype(jnp.bfloat16), value_block,
        preferred_element_type=jnp.float32,
    )
    return (weighted, peaks, totals)


def merge_all(parts):
    peaks = [jnp.where(p[2] > 0, p[1], MASKED_SCORE) for p in parts]
    top = peaks[0]
    for pk in peaks[1:]:
        top = jnp.maximum(top, pk)
    weighted = 0.0
    totals = 0.0
    for part, pk in zip(parts, peaks):
        scale = jnp.where(part[2] > 0, jnp.exp(pk - top), 0.0)
        weighted = weighted + part[0] * scale[..., None]
        totals = totals + part[2] * scale
    return (weighted, top, totals)


def pack(part):
    weighted, peaks, totals = part
    n = weighted.shape[0]
    return jnp.concatenate(
        [weighted.reshape(n, -1), peaks.reshape(n, -1), totals.reshape(n, -1)], axis=1
    )


def unpack(packed, shape):
    n, k, g, d = shape
    width = k * g * d
    weighted = packed[:, :width].reshape(n, k, g, d)
    peaks = packed[:, width : width + k * g].reshape(n, k, g)
    totals = packed[:, width + k * g :].reshape(n, k, g)
    return (weighted, peaks, totals)


def swapped(block, axis):
    devices = range(lax.axis_size(axis))
    return lax.ppermute(block, axis, [(i, i ^ 1) for i in devices])


def local(queries, new_kv, own_kv, prompt_kv, out_weight, parents, own_len, first_beam):
    per_dev = queries.shape[0]
    head_dim = HD
    kv_heads_local = new_kv.shape[2] // head_dim
    q_heads_local = queries.shape[1] // head_dim
    group_size = q_heads_local // kv_heads_local
    own_size = own_kv.shape[1]
    prompt_size = prompt_kv.shape[1]
    req_count = lax.axis_size("req")
    beam_count = per_dev * req_count
    dev_index = lax.axis_index("req")
    mate_index = dev_index ^ 1
    chip = dev_index // 2
    shape4 = (per_dev, kv_heads_local, group_size, head_dim)
    cache_rows = per_dev * own_size

    local_rows = jnp.concatenate(
        [own_kv.reshape(cache_rows, 2, -1), prompt_kv[0]], axis=0
    )
    local_kv = jnp.moveaxis(local_rows, 1, 0)
    mate_kv = swapped(local_kv, "req")

    from_prev = shifted(queries, "req", -2)
    from_next = shifted(queries, "req", 2)
    hood_queries = jnp.concatenate([from_prev, from_next, queries], axis=0)
    hood_queries = hood_queries.reshape((3 * per_dev,) + shape4[1:])
    query_block = queries.reshape(shape4)
    hood_count = 3 * per_dev
    slot_ids = jnp.arange(per_dev, dtype=jnp.int32)
    hood_beams = jnp.concatenate(
        [(dev_index + k) * per_dev + slot_ids for k in (-2, 2, 0)]
    )
    in_range = (hood_beams >= 0) & (hood_beams < beam_count)
    pad = 2 * per_dev
    index_rows = jnp.pad(jnp.stack([parents, first_beam, own_len]), ((0, 0), (pad, pad)))
    window = lax.dynamic_slice_in_dim(index_rows, dev_index * per_dev, 5 * per_dev, axis=1)
    hood_index = jnp.concatenate(
        [window[:, 0:per_dev], window[:, 4 * per_dev :], window[:, 2 * per_dev : 3 * per_dev]],
        axis=1,
    )
    parent = hood_index[0]
    home = hood_index[1] // per_dev
    local_len = window[2, pad : pad + per_dev]
    mate_len = lax.dynamic_slice_in_dim(
        window[2], 3 * per_dev - 2 * per_dev * (dev_index % 2), per_dev
    )
    parent_dev = parent // per_dev
    columns = jnp.arange(cache_rows, dtype=jnp.int32)
    column_slot = columns // own_size

    kv_count = cache_rows + prompt_size
    all_columns = jnp.arange(kv_count, dtype=jnp.int32)
    is_cache = all_columns < cache_rows
    column_slot = all_columns // own_size
    column_pos = all_columns % own_size

    def allowed_for(holder, lengths):
        per_column = jnp.broadcast_to(lengths[:, None], (per_dev, own_size)).reshape(-1)
        column_len = jnp.pad(per_column, (0, prompt_size))
        own_ok = (
            (in_range & (parent_dev == holder))[:, None]
            & is_cache[None, :]
            & (column_slot[None, :] == (parent % per_dev)[:, None])
            & (column_pos < column_len)[None, :]
        )
        prompt_ok = (in_range & (home == holder))[:, None] & ~is_cache[None, :]
        return own_ok | prompt_ok

    sent = 2 * per_dev

    send_parts = []
    own_parts = []
    for kv, holder, lengths in ((local_kv, dev_index, local_len), (mate_kv, mate_index, mate_len)):
        keys = kv[0].reshape(kv_count, kv_heads_local, head_dim)
        values = kv[1].reshape(kv_count, kv_heads_local, head_dim)
        allowed = allowed_for(holder, lengths)
        send_parts.append(partial_block(hood_queries[:sent], keys, values, allowed[:sent]))
        own_parts.append(partial_block(hood_queries[sent:], keys, values, allowed[sent:]))
    send_part = merge_all(send_parts)

    fresh_keys = new_kv[:, 0].reshape(per_dev, 1, kv_heads_local, head_dim)
    fresh_values = new_kv[:, 1].reshape(per_dev, 1, kv_heads_local, head_dim)
    fresh_scores = jnp.einsum(
        "nkgd,nskd->nkgs", query_block, fresh_keys, preferred_element_type=jnp.float32
    ) * (head_dim ** (-0.5))
    fresh_part = (
        fresh_values[:, 0, :, None, :].astype(jnp.float32) * jnp.ones_like(fresh_scores),
        fresh_scores[..., 0],
        jnp.ones_like(fresh_scores[..., 0]),
    )

    def rows(part, lo):
        return tuple(x[lo : lo + per_dev] for x in part)

    back_from_next = unpack(shifted(pack(rows(send_part, 0)), "req", 2), shape4)
    back_from_prev = unpack(shifted(pack(rows(send_part, per_dev)), "req", -2), shape4)
    weighted, _, totals = merge_all(
        [fresh_part] + own_parts + [back_from_next, back_from_prev]
    )
    attended = (
        (weighted / totals[..., None])
        .reshape(per_dev, q_heads_local * head_dim)
        .astype(jnp.bfloat16)
    )
    partial_term = jnp.dot(attended, out_weight, preferred_element_type=jnp.float32)

    tp_count = lax.axis_size("tp")
    tp_index = lax.axis_index("tp")
    width = partial_term.shape[1] // tp_count
    chunks = partial_term.reshape(per_dev, tp_count, width).transpose(1, 0, 2)
    got = lax.all_to_all(chunks.astype(jnp.bfloat16), "tp", 0, 0, tiled=True)
    others = jnp.arange(tp_count, dtype=jnp.int32)[:, None, None] != tp_index
    mine = lax.dynamic_slice_in_dim(partial_term, tp_index * width, width, axis=1)
    total = mine + jnp.sum(jnp.where(others, got.astype(jnp.float32), 0.0), axis=0)
    return total.astype(jnp.bfloat16)


def solution(mesh):
    in_specs = (
        P("req", "tp"),
        P("req", None, "tp"),
        P("req", None, None, "tp"),
        P("req", None, None, "tp"),
        P("tp", None),
        P(),
        P(),
        P(),
    )
    out_specs = P("req", "tp")
    return jax.shard_map(local, mesh=mesh, in_specs=in_specs, out_specs=out_specs, check_vma=False)
```

```python
import jax
import jax.numpy as jnp
from jax import lax
from jax.sharding import PartitionSpec as P

HD = 128
MOST_BEAMS = 16


MASKED_SCORE = -1e30


def shifted(block, axis, distance):
    devices = range(lax.axis_size(axis))
    route = [(i + distance, i) for i in devices if i + distance in devices]
    return lax.ppermute(block, axis, route)


def softmax_block(query_block, key_block, allowed):
    score_scale = query_block.shape[-1] ** (-0.5)
    scores = jnp.einsum(
        "nkgd,skd->nkgs", query_block, key_block, preferred_element_type=jnp.float32
    )
    scores = scores * score_scale
    masked = allowed[:, None, None, :]
    scores = jnp.where(masked, scores, MASKED_SCORE)
    peaks = jnp.max(scores, axis=-1)
    weights = jnp.where(masked, jnp.exp(scores - peaks[..., None]), 0.0)
    return weights.astype(jnp.bfloat16), peaks, jnp.sum(weights, axis=-1)


def weigh(weights, value_block):
    return jnp.einsum("nkgs,skd->nkgd", weights, value_block, preferred_element_type=jnp.float32)


def partial_block(query_block, key_block, value_block, allowed):
    score_scale = query_block.shape[-1] ** (-0.5)
    scores = jnp.einsum(
        "nkgd,skd->nkgs", query_block, key_block, preferred_element_type=jnp.float32
    )
    scores = scores * score_scale
    masked = allowed[:, None, None, :]
    scores = jnp.where(masked, scores, MASKED_SCORE)
    peaks = jnp.max(scores, axis=-1)
    weights = jnp.where(masked, jnp.exp(scores - peaks[..., None]), 0.0)
    totals = jnp.sum(weights, axis=-1)
    weighted = jnp.einsum(
        "nkgs,skd->nkgd", weights.astype(jnp.bfloat16), value_block,
        preferred_element_type=jnp.float32,
    )
    return (weighted, peaks, totals)


def merge_all(parts):
    peaks = [jnp.where(p[2] > 0, p[1], MASKED_SCORE) for p in parts]
    top = peaks[0]
    for pk in peaks[1:]:
        top = jnp.maximum(top, pk)
    weighted = 0.0
    totals = 0.0
    for part, pk in zip(parts, peaks):
        scale = jnp.where(part[2] > 0, jnp.exp(pk - top), 0.0)
        weighted = weighted + part[0] * scale[..., None]
        totals = totals + part[2] * scale
    return (weighted, top, totals)


def pack(part):
    weighted, peaks, totals = part
    n = weighted.shape[0]
    return jnp.concatenate(
        [weighted.reshape(n, -1), peaks.reshape(n, -1), totals.reshape(n, -1)], axis=1
    )


def unpack(packed, shape):
    n, k, g, d = shape
    width = k * g * d
    weighted = packed[:, :width].reshape(n, k, g, d)
    peaks = packed[:, width : width + k * g].reshape(n, k, g)
    totals = packed[:, width + k * g :].reshape(n, k, g)
    return (weighted, peaks, totals)


def swapped(block, axis):
    devices = range(lax.axis_size(axis))
    return lax.ppermute(block, axis, [(i, i ^ 1) for i in devices])


def local(queries, new_kv, own_kv, prompt_kv, out_weight, parents, own_len, first_beam):
    per_dev = queries.shape[0]
    head_dim = HD
    kv_heads_local = new_kv.shape[2] // head_dim
    q_heads_local = queries.shape[1] // head_dim
    group_size = q_heads_local // kv_heads_local
    own_size = own_kv.shape[1]
    prompt_size = prompt_kv.shape[1]
    req_count = lax.axis_size("req")
    beam_count = per_dev * req_count
    dev_index = lax.axis_index("req")
    mate_index = dev_index ^ 1
    chip = dev_index // 2
    shape4 = (per_dev, kv_heads_local, group_size, head_dim)
    cache_rows = per_dev * own_size

    local_rows = jnp.concatenate(
        [own_kv.reshape(cache_rows, 2, -1), prompt_kv[0]], axis=0
    )
    local_kv = jnp.moveaxis(local_rows, 1, 0)
    mate_kv = swapped(local_kv, "req")

    from_prev = shifted(queries, "req", -2)
    from_next = shifted(queries, "req", 2)
    hood_queries = jnp.concatenate([from_prev, from_next, queries], axis=0)
    hood_queries = hood_queries.reshape((3 * per_dev,) + shape4[1:])
    query_block = queries.reshape(shape4)
    hood_count = 3 * per_dev
    slot_ids = jnp.arange(per_dev, dtype=jnp.int32)
    hood_beams = jnp.concatenate(
        [(dev_index + k) * per_dev + slot_ids for k in (-2, 2, 0)]
    )
    in_range = (hood_beams >= 0) & (hood_beams < beam_count)
    pad = 2 * per_dev
    index_rows = jnp.pad(jnp.stack([parents, first_beam, own_len]), ((0, 0), (pad, pad)))
    window = lax.dynamic_slice_in_dim(index_rows, dev_index * per_dev, 5 * per_dev, axis=1)
    hood_index = jnp.concatenate(
        [window[:, 0:per_dev], window[:, 4 * per_dev :], window[:, 2 * per_dev : 3 * per_dev]],
        axis=1,
    )
    parent = hood_index[0]
    home = hood_index[1] // per_dev
    local_len = window[2, pad : pad + per_dev]
    mate_len = lax.dynamic_slice_in_dim(
        window[2], 3 * per_dev - 2 * per_dev * (dev_index % 2), per_dev
    )
    parent_dev = parent // per_dev
    columns = jnp.arange(cache_rows, dtype=jnp.int32)
    column_slot = columns // own_size

    kv_count = cache_rows + prompt_size
    all_columns = jnp.arange(kv_count, dtype=jnp.int32)
    is_cache = all_columns < cache_rows
    column_slot = all_columns // own_size
    column_pos = all_columns % own_size

    def allowed_for(holder, lengths):
        per_column = jnp.broadcast_to(lengths[:, None], (per_dev, own_size)).reshape(-1)
        column_len = jnp.pad(per_column, (0, prompt_size))
        own_ok = (
            (in_range & (parent_dev == holder))[:, None]
            & is_cache[None, :]
            & (column_slot[None, :] == (parent % per_dev)[:, None])
            & (column_pos < column_len)[None, :]
        )
        prompt_ok = (in_range & (home == holder))[:, None] & ~is_cache[None, :]
        return own_ok | prompt_ok

    sent = 2 * per_dev

    send_parts = []
    own_parts = []
    for kv, holder, lengths in ((local_kv, dev_index, local_len), (mate_kv, mate_index, mate_len)):
        keys = kv[0].reshape(kv_count, kv_heads_local, head_dim)
        values = kv[1].reshape(kv_count, kv_heads_local, head_dim)
        allowed = allowed_for(holder, lengths)
        weights, peaks, totals = softmax_block(hood_queries, keys, allowed)
        send_parts.append((weigh(weights[:sent], values), peaks[:sent], totals[:sent]))
        own_parts.append((weigh(weights[sent:], values), peaks[sent:], totals[sent:]))
    send_part = merge_all(send_parts)

    fresh_keys = new_kv[:, 0].reshape(per_dev, 1, kv_heads_local, head_dim)
    fresh_values = new_kv[:, 1].reshape(per_dev, 1, kv_heads_local, head_dim)
    fresh_scores = jnp.einsum(
        "nkgd,nskd->nkgs", query_block, fresh_keys, preferred_element_type=jnp.float32
    ) * (head_dim ** (-0.5))
    fresh_part = (
        fresh_values[:, 0, :, None, :].astype(jnp.float32) * jnp.ones_like(fresh_scores),
        fresh_scores[..., 0],
        jnp.ones_like(fresh_scores[..., 0]),
    )

    def rows(part, lo):
        return tuple(x[lo : lo + per_dev] for x in part)

    back_from_next = unpack(shifted(pack(rows(send_part, 0)), "req", 2), shape4)
    back_from_prev = unpack(shifted(pack(rows(send_part, per_dev)), "req", -2), shape4)
    weighted, _, totals = merge_all(
        [fresh_part] + own_parts + [back_from_next, back_from_prev]
    )
    attended = (
        (weighted / totals[..., None])
        .reshape(per_dev, q_heads_local * head_dim)
        .astype(jnp.bfloat16)
    )
    half = out_weight.shape[1] // 2
    partial_term = jnp.concatenate(
        [
            jnp.dot(attended, out_weight[:, :half], preferred_element_type=jnp.float32),
            jnp.dot(attended, out_weight[:, half:], preferred_element_type=jnp.float32),
        ],
        axis=1,
    )

    tp_count = lax.axis_size("tp")
    tp_index = lax.axis_index("tp")
    width = partial_term.shape[1] // tp_count
    chunks = partial_term.reshape(per_dev, tp_count, width).transpose(1, 0, 2)
    got = lax.all_to_all(chunks.astype(jnp.bfloat16), "tp", 0, 0, tiled=True)
    others = jnp.arange(tp_count, dtype=jnp.int32)[:, None, None] != tp_index
    mine = lax.dynamic_slice_in_dim(partial_term, tp_index * width, width, axis=1)
    total = mine + jnp.sum(jnp.where(others, got.astype(jnp.float32), 0.0), axis=0)
    return total.astype(jnp.bfloat16)


def solution(mesh):
    in_specs = (
        P("req", "tp"),
        P("req", None, "tp"),
        P("req", None, None, "tp"),
        P("req", None, None, "tp"),
        P("tp", None),
        P(),
        P(),
        P(),
    )
    out_specs = P("req", "tp")
    return jax.shard_map(local, mesh=mesh, in_specs=in_specs, out_specs=out_specs, check_vma=False)
```

```python
import jax
import jax.numpy as jnp
from jax import lax
from jax.sharding import PartitionSpec as P

HD = 128
MOST_BEAMS = 16


MASKED_SCORE = -1e30


def shifted(block, axis, distance):
    devices = range(lax.axis_size(axis))
    route = [(i + distance, i) for i in devices if i + distance in devices]
    return lax.ppermute(block, axis, route)


def partial_block(query_block, key_block, value_block, allowed):
    score_scale = query_block.shape[-1] ** (-0.5)
    scores = jnp.einsum(
        "nkgd,skd->nkgs", query_block, key_block, preferred_element_type=jnp.float32
    )
    scores = scores * score_scale
    masked = allowed[:, None, None, :]
    scores = jnp.where(masked, scores, MASKED_SCORE)
    peaks = jnp.max(scores, axis=-1)
    weights = jnp.where(masked, jnp.exp(scores - peaks[..., None]), 0.0)
    totals = jnp.sum(weights, axis=-1)
    weighted = jnp.einsum(
        "nkgs,skd->nkgd", weights.astype(jnp.bfloat16), value_block,
        preferred_element_type=jnp.float32,
    )
    return (weighted, peaks, totals)


def merge_all(parts):
    peaks = [jnp.where(p[2] > 0, p[1], MASKED_SCORE) for p in parts]
    top = peaks[0]
    for pk in peaks[1:]:
        top = jnp.maximum(top, pk)
    weighted = 0.0
    totals = 0.0
    for part, pk in zip(parts, peaks):
        scale = jnp.where(part[2] > 0, jnp.exp(pk - top), 0.0)
        weighted = weighted + part[0] * scale[..., None]
        totals = totals + part[2] * scale
    return (weighted, top, totals)


def pack(part):
    weighted, peaks, totals = part
    n = weighted.shape[0]
    return jnp.concatenate(
        [weighted.reshape(n, -1), peaks.reshape(n, -1), totals.reshape(n, -1)], axis=1
    )


def unpack(packed, shape):
    n, k, g, d = shape
    width = k * g * d
    weighted = packed[:, :width].reshape(n, k, g, d)
    peaks = packed[:, width : width + k * g].reshape(n, k, g)
    totals = packed[:, width + k * g :].reshape(n, k, g)
    return (weighted, peaks, totals)


def swapped(block, axis):
    devices = range(lax.axis_size(axis))
    return lax.ppermute(block, axis, [(i, i ^ 1) for i in devices])


def local(queries, new_kv, own_kv, prompt_kv, out_weight, parents, own_len, first_beam):
    per_dev = queries.shape[0]
    head_dim = HD
    kv_heads_local = new_kv.shape[2] // head_dim
    q_heads_local = queries.shape[1] // head_dim
    group_size = q_heads_local // kv_heads_local
    own_size = own_kv.shape[1]
    prompt_size = prompt_kv.shape[1]
    req_count = lax.axis_size("req")
    beam_count = per_dev * req_count
    dev_index = lax.axis_index("req")
    mate_index = dev_index ^ 1
    chip = dev_index // 2
    shape4 = (per_dev, kv_heads_local, group_size, head_dim)
    cache_rows = per_dev * own_size

    local_rows = jnp.concatenate(
        [own_kv.reshape(cache_rows, 2, -1), prompt_kv[0]], axis=0
    )
    local_kv = jnp.moveaxis(local_rows, 1, 0)
    mate_kv = swapped(local_kv, "req")

    from_prev = shifted(queries, "req", -2)
    from_next = shifted(queries, "req", 2)
    hood_queries = jnp.concatenate([from_prev, queries, from_next], axis=0)
    hood_queries = hood_queries.reshape((3 * per_dev,) + shape4[1:])
    query_block = queries.reshape(shape4)
    hood_count = 3 * per_dev
    slot_ids = jnp.arange(per_dev, dtype=jnp.int32)
    hood_beams = jnp.concatenate(
        [(dev_index + k) * per_dev + slot_ids for k in (-2, 0, 2)]
    )
    in_range = (hood_beams >= 0) & (hood_beams < beam_count)
    pad = 2 * per_dev
    index_rows = jnp.pad(jnp.stack([parents, first_beam, own_len]), ((0, 0), (pad, pad)))
    window = lax.dynamic_slice_in_dim(index_rows, dev_index * per_dev, 5 * per_dev, axis=1)
    hood_index = jnp.concatenate(
        [window[:, 0:per_dev], window[:, 2 * per_dev : 3 * per_dev], window[:, 4 * per_dev :]],
        axis=1,
    )
    parent = hood_index[0]
    home = hood_index[1] // per_dev
    local_len = window[2, pad : pad + per_dev]
    mate_len = lax.dynamic_slice_in_dim(
        window[2], 3 * per_dev - 2 * per_dev * (dev_index % 2), per_dev
    )
    parent_dev = parent // per_dev
    columns = jnp.arange(cache_rows, dtype=jnp.int32)
    column_slot = columns // own_size

    kv_count = cache_rows + prompt_size
    all_columns = jnp.arange(kv_count, dtype=jnp.int32)
    is_cache = all_columns < cache_rows
    column_slot = all_columns // own_size
    column_pos = all_columns % own_size

    def allowed_for(holder, lengths):
        per_column = jnp.broadcast_to(lengths[:, None], (per_dev, own_size)).reshape(-1)
        column_len = jnp.pad(per_column, (0, prompt_size))
        own_ok = (
            (in_range & (parent_dev == holder))[:, None]
            & is_cache[None, :]
            & (column_slot[None, :] == (parent % per_dev)[:, None])
            & (column_pos < column_len)[None, :]
        )
        prompt_ok = (in_range & (home == holder))[:, None] & ~is_cache[None, :]
        return own_ok | prompt_ok

    parts_here = []
    for kv, holder, lengths in ((local_kv, dev_index, local_len), (mate_kv, mate_index, mate_len)):
        keys = kv[0].reshape(kv_count, kv_heads_local, head_dim)
        values = kv[1].reshape(kv_count, kv_heads_local, head_dim)
        parts_here.append(partial_block(hood_queries, keys, values, allowed_for(holder, lengths)))
    hood_part = merge_all(parts_here)

    fresh_keys = new_kv[:, 0].reshape(per_dev, 1, kv_heads_local, head_dim)
    fresh_values = new_kv[:, 1].reshape(per_dev, 1, kv_heads_local, head_dim)
    fresh_scores = jnp.einsum(
        "nkgd,nskd->nkgs", query_block, fresh_keys, preferred_element_type=jnp.float32
    ) * (head_dim ** (-0.5))
    fresh_part = (
        fresh_values[:, 0, :, None, :].astype(jnp.float32) * jnp.ones_like(fresh_scores),
        fresh_scores[..., 0],
        jnp.ones_like(fresh_scores[..., 0]),
    )

    def rows(part, lo):
        return tuple(x[lo : lo + per_dev] for x in part)

    back_from_next = unpack(shifted(pack(rows(hood_part, 0)), "req", 2), shape4)
    back_from_prev = unpack(shifted(pack(rows(hood_part, 2 * per_dev)), "req", -2), shape4)
    weighted, _, totals = merge_all(
        [fresh_part, rows(hood_part, per_dev), back_from_next, back_from_prev]
    )
    attended = (
        (weighted / totals[..., None])
        .reshape(per_dev, q_heads_local * head_dim)
        .astype(jnp.bfloat16)
    )
    partial_term = jnp.dot(attended, out_weight, preferred_element_type=jnp.float32)

    tp_count = lax.axis_size("tp")
    width = partial_term.shape[1] // tp_count
    chunks = partial_term.astype(jnp.bfloat16).reshape(per_dev, tp_count, width)
    got = lax.all_to_all(chunks, "tp", 1, 1, tiled=True)
    return jnp.sum(got.astype(jnp.float32), axis=1).astype(jnp.bfloat16)


def solution(mesh):
    in_specs = (
        P("req", "tp"),
        P("req", None, "tp"),
        P("req", None, None, "tp"),
        P("req", None, None, "tp"),
        P("tp", None),
        P(),
        P(),
        P(),
    )
    out_specs = P("req", "tp")
    return jax.shard_map(local, mesh=mesh, in_specs=in_specs, out_specs=out_specs, check_vma=False)
```
